32 devices in a mesh: ind: 8 (over z, x), var: 4 (over y, core).
Axes of the slice: x: 2, y: 2, z: 4, core: 2. Of those that a mesh axis runs over, the one named last changes fastest.
Arguments:
- genotypes: float32 [256, 16384], P('var', 'ind'), may hold values from -30 to 30
- variance_comp: float32 [2], replicated, may hold values from 0.5 to 1.5
- grm_tiles: bfloat16 [80, 512, 512], P('ind'), may hold values from -1 to 6, as said below
- tile_rows: int32 [80], P('ind'), may hold values from 0 to 3, as said below
- tile_cols: int32 [80], P('ind'), may hold values from 0 to 31, as said below
- tile_live: int32 [8], P('ind'), may hold values from 5 to 10, as said below
Outputs:
- solution: float32 [256, 16384], P('var', 'ind')
- gene_gram: float32 [256, 4], P('var')
The draws below stay inside these ranges and needn't reach their ends.
Inputs may be any that keep to these rules, and one draw needn't show every extreme that they name: `grm_tiles`: every diagonal tile is symmetric, and the tiles of two live slots that form a transposed pair are transposes of each other, so K is symmetric. Slots r < 4 of each index i of ind hold its diagonal tiles: tile_rows = r and tile_cols = i * 4 + r. `tile_cols`: every other slot of index i names a column tile j * 4 + ((i + t) mod 4) of another index j != i, with t < 2. Live off slots come in transposed pairs: a live slot of i at row tile r naming column tile j * 4 + u goes with a live slot of j at row tile u naming column tile i * 4 + r. Some index uses 2 distinct column tiles of one other index. `tile_live`: some index of ind uses all 10 slots.
All inputs are finite; a program needn't handle non-finite values.
Results may differ from the reference program's by a relative error of at most 0.0003.
Values sent between devices are 32-bit elements; how exact they have to be, the bound alone decides.
No kernel may reach another device: no remote copies, remote signals or barrier semaphores. Data moves between devices by JAX's collectives and lax.ppermute only.
A program may use at most 192 MiB of HBM per device.

```python
import jax
import jax.numpy as jnp
from jax import lax

COLS = 256
VARS_GENE = 4
GENES = 64
TILE = 512
RT_DEV = 4
OFF_DEV = 6
ITERS = 2
NEED = 2
TILES_DEV = 10
IND = 16384
N_IND = 8


def pattern(key):
    owners = IND // (RT_DEV * TILE)
    half_count = owners // 2
    keys = jax.random.split(jax.random.fold_in(key, 7), 4 + OFF_DEV)
    owner_ids = jnp.arange(owners, dtype=jnp.int32)
    busiest = jax.random.randint(keys[0], (), 0, owners, dtype=jnp.int32)
    first_offset = jax.random.randint(keys[1], (OFF_DEV, half_count), 0, NEED, dtype=jnp.int32)
    second_offset = jax.random.randint(keys[2], (OFF_DEV, half_count), 0, NEED, dtype=jnp.int32)
    coins = jax.random.randint(keys[3], (OFF_DEV, half_count), 0, 2, dtype=jnp.int32)
    mates = []
    pair_ids = []
    firsts = []
    for rounds in range(OFF_DEV):
        if rounds < NEED:
            relative = (owner_ids - busiest) % owners
            mate = (busiest + (relative ^ 1)) % owners
            pair_here = relative // 2
            first_here = relative % 2 == 0
        else:
            order = jax.random.permutation(keys[4 + rounds], owners).astype(jnp.int32)
            place = jnp.zeros((owners,), jnp.int32).at[order].set(owner_ids)
            mate = order[place ^ 1]
            pair_here = place // 2
            first_here = place % 2 == 0
        mates.append(mate)
        pair_ids.append(pair_here)
        firsts.append(first_here)
    mate = jnp.stack(mates)
    pair_id = jnp.stack(pair_ids)
    first = jnp.stack(firsts)
    round_ids = jnp.arange(OFF_DEV, dtype=jnp.int32)[:, None]
    forced_pair = (round_ids < NEED) & (jnp.arange(half_count, dtype=jnp.int32)[None, :] == 0)
    first_offset = jnp.where(forced_pair, jnp.broadcast_to(round_ids, (OFF_DEV, half_count)), first_offset)
    active_pair = (coins == 1) | (round_ids == 0)
    active = jnp.take_along_axis(active_pair, pair_id, axis=1)
    active = active | (owner_ids[None, :] == busiest) | (mate == busiest)
    off_first = jnp.take_along_axis(first_offset, pair_id, axis=1)
    off_second = jnp.take_along_axis(second_offset, pair_id, axis=1)
    own_offset = jnp.where(first, off_first, off_second)
    mate_offset = jnp.where(first, off_second, off_first)
    rows_off = (mate + mate_offset) % RT_DEV
    cols_off = mate * RT_DEV + (owner_ids[None, :] + own_offset) % RT_DEV
    score = (1 - active.astype(jnp.int32)) * OFF_DEV + round_ids
    score = jnp.transpose(score)
    order_slots = jnp.argsort(score, axis=1, stable=True).astype(jnp.int32)
    rows_off = jnp.take_along_axis(jnp.transpose(rows_off), order_slots, axis=1)
    cols_off = jnp.take_along_axis(jnp.transpose(cols_off), order_slots, axis=1)
    pair_sorted = jnp.take_along_axis(jnp.transpose(pair_id), order_slots, axis=1)
    first_sorted = jnp.take_along_axis(jnp.transpose(first), order_slots, axis=1)
    live = RT_DEV + jnp.sum(active.astype(jnp.int32), axis=0)
    diag_rows = jnp.broadcast_to(jnp.arange(RT_DEV, dtype=jnp.int32)[None, :], (owners, RT_DEV))
    diag_cols = owner_ids[:, None] * RT_DEV + diag_rows
    rows = jnp.concatenate([diag_rows, rows_off], axis=1).reshape(-1)
    cols = jnp.concatenate([diag_cols, cols_off], axis=1).reshape(-1)
    return (rows, cols, live, order_slots, pair_sorted, first_sorted)


def membership(rows, live):
    owners = IND // (RT_DEV * TILE)
    rows_off = rows.reshape(owners, TILES_DEV)[:, RT_DEV:]
    live_off = (jnp.arange(OFF_DEV, dtype=jnp.int32)[None, :] < (live - RT_DEV)[:, None]).astype(jnp.float32)
    member = (rows_off[:, :, None] == jnp.arange(RT_DEV, dtype=jnp.int32)[None, None, :]).astype(jnp.float32)
    return member * live_off[:, :, None]


def draw_tile_rows(key, part):
    return pattern(key)[0]


def draw_tile_cols(key, part):
    return pattern(key)[1]


def draw_tile_live(key, part):
    return pattern(key)[2]


def draw_grm_tiles(key, part):
    owners = IND // (RT_DEV * TILE)
    half_count = owners // 2
    rows, cols, live, order_slots, pair_sorted, first_sorted = pattern(key)
    member = membership(rows, live)
    keys = jax.random.split(jax.random.fold_in(key, 11), 4)
    spread = 0.25 / (TILE * TILES_DEV) ** 0.5
    pair_noise = jax.random.truncated_normal(keys[0], -5.0, 5.0, (OFF_DEV, half_count, TILE, TILE), jnp.float32) * spread
    diag_noise = jax.random.truncated_normal(keys[2], -5.0, 5.0, (owners, RT_DEV, TILE, TILE), jnp.float32) * spread
    diag_noise = (diag_noise + jnp.swapaxes(diag_noise, 2, 3)) * 0.7071
    kinship = jax.random.uniform(keys[3], (OFF_DEV, half_count, TILE), jnp.float32, 0.3, 0.6)
    chosen_kin = kinship[order_slots, pair_sorted]
    kin_total = jnp.zeros((owners, RT_DEV, TILE), jnp.float32)
    for slot in range(OFF_DEV):
        kin_total = kin_total + member[:, slot, :, None] * chosen_kin[:, slot, None, :]
    base_values = jnp.exp(jax.random.uniform(keys[1], (owners, RT_DEV, TILE), jnp.float32, -0.9163, 0.47))
    diag_values = base_values + kin_total
    identity = jnp.arange(TILE)[:, None] == jnp.arange(TILE)[None, :]
    diag_tiles = jnp.where(identity[None, None, :, :], diag_values[:, :, :, None], diag_noise)
    chosen = pair_noise[order_slots, pair_sorted]
    off_tiles = jnp.where(first_sorted[:, :, None, None], chosen, jnp.swapaxes(chosen, 2, 3))
    off_tiles = off_tiles + jnp.where(identity[None, None, :, :], chosen_kin[:, :, :, None], 0.0)
    tiles = jnp.concatenate([diag_tiles, off_tiles], axis=1).reshape(owners * TILES_DEV, TILE, TILE)
    return tiles.astype(jnp.bfloat16)


def draw_genotypes(key, part):
    owners = IND // (RT_DEV * TILE)
    half_count = owners // 2
    rows, cols, live, order_slots, pair_sorted, first_sorted = pattern(key)
    member = membership(rows, live)
    keys = jax.random.split(jax.random.fold_in(key, 3), 3)
    position = jnp.arange(IND, dtype=jnp.float32) / IND
    rising = 3.0 ** position
    noise = jax.random.truncated_normal(keys[0], -3.0, 3.0, (COLS, owners, RT_DEV, TILE), jnp.float32)
    shared = jax.random.truncated_normal(keys[2], -3.0, 3.0, (OFF_DEV, half_count, COLS, TILE), jnp.float32)
    total = noise
    count = jnp.zeros((owners, RT_DEV), jnp.float32)
    for slot in range(OFF_DEV):
        piece = shared[order_slots[:, slot], pair_sorted[:, slot]]
        weight = member[:, slot, :]
        total = total + jnp.transpose(piece, (1, 0, 2))[:, :, None, :] * weight[None, :, :, None]
        count = count + weight
    core = total / jnp.sqrt(1.0 + count)[None, :, :, None]
    core = core.reshape(COLS, IND)
    values = core * rising[None, :]
    return values


def setup_inputs(seed: int = 0) -> dict:
    seeds = jax.random.split(jax.random.key(seed), 7)
    genotypes = draw_genotypes(jax.random.fold_in(seeds[6], 71), 0)
    variance_comp = jnp.clip(jax.random.uniform(seeds[1], (2,), jnp.float32, 0.5, 1.5), 0.5, 1.5)
    grm_tiles = draw_grm_tiles(jax.random.fold_in(seeds[6], 71), 0)
    tile_rows = draw_tile_rows(jax.random.fold_in(seeds[6], 71), 0)
    tile_cols = draw_tile_cols(jax.random.fold_in(seeds[6], 71), 0)
    tile_live = draw_tile_live(jax.random.fold_in(seeds[6], 71), 0)
    return {"genotypes": genotypes, "variance_comp": variance_comp, "grm_tiles": grm_tiles, "tile_rows": tile_rows, "tile_cols": tile_cols, "tile_live": tile_live}


def tile_product(direction, grm_tiles, tile_rows, tile_cols, tile_live):
    blocks = direction.reshape(COLS, RT_DEV * N_IND, TILE)
    tiles_all = grm_tiles.reshape(N_IND, TILES_DEV, TILE, TILE)
    rows_all = tile_rows.reshape(N_IND, TILES_DEV)
    cols_all = tile_cols.reshape(N_IND, TILES_DEV)

    def owner_rows(pieces):
        tiles_here, rows_here, cols_here, live_here = pieces
        picked = jnp.take(blocks, cols_here.astype(jnp.int32), axis=1)
        product = jnp.einsum("csk,sqk->csq", picked, tiles_here.astype(jnp.float32),
                             precision=lax.Precision.HIGHEST)
        live_mask = (jnp.arange(TILES_DEV, dtype=jnp.int32) < live_here).astype(jnp.float32)
        onehot = (rows_here[:, None] == jnp.arange(RT_DEV, dtype=jnp.int32)[None, :]).astype(jnp.float32)
        onehot = onehot * live_mask[:, None]
        return jnp.einsum("csq,sr->crq", product, onehot, precision=lax.Precision.HIGHEST)

    result = lax.map(owner_rows, (tiles_all, rows_all, cols_all, tile_live))
    return jnp.transpose(result, (1, 0, 2, 3)).reshape(COLS, IND)


def reference(genotypes, variance_comp, grm_tiles, tile_rows, tile_cols, tile_live):
    tau_noise = variance_comp[0]
    tau_kin = variance_comp[1]
    tiles_all = grm_tiles.reshape(N_IND, TILES_DEV, TILE, TILE)
    diag_values = jnp.diagonal(tiles_all[:, :RT_DEV], axis1=2, axis2=3).astype(jnp.float32).reshape(IND)
    precond = tau_noise + tau_kin * diag_values

    def apply(vectors):
        return tau_noise * vectors + tau_kin * tile_product(vectors, grm_tiles, tile_rows, tile_cols, tile_live)

    solution = jnp.zeros_like(genotypes)
    resid = genotypes
    scaled = resid / precond[None, :]
    direction = scaled
    rz_now = jnp.sum(resid * scaled, axis=1)
    for rounds in range(ITERS):
        image = apply(direction)
        alpha = rz_now / jnp.sum(direction * image, axis=1)
        solution = solution + alpha[:, None] * direction
        resid = resid - alpha[:, None] * image
        if rounds + 1 < ITERS:
            scaled = resid / precond[None, :]
            rz_next = jnp.sum(resid * scaled, axis=1)
            direction = scaled + (rz_next / rz_now)[:, None] * direction
            rz_now = rz_next
    geno_split = genotypes.reshape(VARS_GENE, GENES, IND)
    sol_split = solution.reshape(VARS_GENE, GENES, IND)
    gram = jnp.einsum("agn,bgn->agb", geno_split, sol_split, precision=lax.Precision.HIGHEST)
    gene_gram = gram.reshape(COLS, VARS_GENE) / IND
    return solution, gene_gram
```

```python
import jax
import jax.numpy as jnp
from jax import lax
from jax.sharding import PartitionSpec as P

VARS_GENE = 4
NEED = 2
HI = lax.Precision.HIGHEST


def tile_dot(x, tile):
    return lax.dot_general(
        x, tile.astype(jnp.float32), (((1,), (1,)), ((), ())),
        precision=HI, preferred_element_type=jnp.float32,
    )


def local(genotypes, variance_comp, grm_tiles, tile_rows, tile_cols, tile_live):
    cols_here, rows_here = genotypes.shape
    tile_size = grm_tiles.shape[1]
    slot_count = grm_tiles.shape[0]
    row_tiles = rows_here // tile_size
    off_count = slot_count - row_tiles
    me = lax.axis_index("ind")
    peers = lax.axis_size("ind")
    v = lax.axis_index("var")
    nvar = lax.axis_size("var")
    ncol = cols_here * nvar
    genes = ncol // VARS_GENE
    total_ind = peers * rows_here
    tau0 = variance_comp[0]
    tau1 = variance_comp[1]
    live = tile_live[0]

    diag_tiles = grm_tiles[:row_tiles]
    off_tiles = grm_tiles[row_tiles:]
    diag_values = jnp.diagonal(diag_tiles, axis1=1, axis2=2).astype(jnp.float32).reshape(rows_here)
    precond = tau0 + tau1 * diag_values
    off_rows = tile_rows[row_tiles:]
    off_cols = tile_cols[row_tiles:]
    live_mask = (jnp.arange(row_tiles, slot_count, dtype=jnp.int32) < live).astype(jnp.float32)
    weight = (off_rows[:, None] == jnp.arange(row_tiles, dtype=jnp.int32)[None, :]).astype(jnp.float32)
    weight = weight * live_mask[:, None]
    position = off_cols // row_tiles * NEED + (off_cols % row_tiles - me) % row_tiles
    position = jnp.clip(position, 0, peers * NEED - 1)

    table = [(p + t) % row_tiles for p in range(peers) for t in range(NEED)]

    def exchange(x):
        pieces = jnp.stack([x[:, k * tile_size:(k + 1) * tile_size] for k in table])
        return lax.all_to_all(pieces, "ind", split_axis=0, concat_axis=0, tiled=True)

    def kprod(x, arrived):
        far = []
        for s in range(off_count):
            picked = lax.dynamic_index_in_dim(arrived, position[s], 0, keepdims=False)
            far.append(tile_dot(picked, off_tiles[s]))
        out = []
        for r in range(row_tiles):
            acc = tile_dot(x[:, r * tile_size:(r + 1) * tile_size], diag_tiles[r])
            for s in range(off_count):
                acc = acc + weight[s, r] * far[s]
            out.append(acc)
        return jnp.concatenate(out, axis=1)

    geno_all = lax.all_gather(genotypes, "var", axis=0, tiled=True)
    first = v * cols_here
    a_out = first // genes
    g0 = first % genes
    geno_sub = jnp.stack(
        [lax.dynamic_slice_in_dim(geno_all, a * genes + g0, cols_here, 0) for a in range(VARS_GENE)]
    )

    z0 = genotypes / precond[None, :]
    arrived0 = exchange(z0)
    kz0 = kprod(z0, arrived0)
    image0 = tau0 * z0 + tau1 * kz0
    w = image0 / precond[None, :]
    arrived1 = exchange(w)

    red1 = lax.psum(jnp.stack([jnp.sum(genotypes * z0, axis=1), jnp.sum(z0 * image0, axis=1)]), "ind")
    rz0 = red1[0]
    alpha0 = rz0 / red1[1]
    resid1 = genotypes - alpha0[:, None] * image0
    z1 = resid1 / precond[None, :]
    rz1 = lax.psum(jnp.sum(resid1 * z1, axis=1), "ind")
    beta = rz1 / rz0
    p0 = jnp.sum(geno_sub * z0[None], axis=2)

    kw = kprod(w, arrived1)
    dir1 = z1 + beta[:, None] * z0
    kdir1 = (kz0 - alpha0[:, None] * kw) + beta[:, None] * kz0
    image1 = tau0 * dir1 + tau1 * kdir1
    dad1 = jnp.sum(dir1 * image1, axis=1)
    pd1 = jnp.sum(geno_sub * dir1[None], axis=2)

    lead = (me == 0).astype(jnp.float32)
    block = jnp.concatenate(
        [dad1[None], (rz1 * lead)[None], alpha0[None] * p0, pd1], axis=0
    )
    nrow = block.shape[0]
    full = jnp.zeros((nrow, nvar, cols_here), jnp.float32)
    full = lax.dynamic_update_slice(full, block[:, None, :], (0, v, 0))
    full = lax.psum(full.reshape(nrow, ncol), ("ind", "var"))
    alpha1_all = full[1] / full[0]
    alpha1 = lax.dynamic_slice_in_dim(alpha1_all, first, cols_here, 0)
    solution = alpha0[:, None] * z0 + alpha1[:, None] * dir1

    a0p0 = lax.dynamic_index_in_dim(full[2:2 + VARS_GENE], a_out, 0, keepdims=False)
    pd1_all = lax.dynamic_index_in_dim(full[2 + VARS_GENE:], a_out, 0, keepdims=False)
    gram_cols = a0p0 + alpha1_all * pd1_all
    gram_cols = lax.dynamic_slice_in_dim(gram_cols.reshape(VARS_GENE, genes), g0, cols_here, 1)
    gene_gram = jnp.transpose(gram_cols) / total_ind
    return (solution, gene_gram)


def solution(mesh):
    placed = (P("var", "ind"), P(), P("ind", None, None), P("ind"), P("ind"), P("ind"))
    return jax.shard_map(
        local,
        mesh=mesh,
        in_specs=placed,
        out_specs=(P("var", "ind"), P("var", None)),
        check_vma=False,
    )
```

```python
import jax
import jax.numpy as jnp
from jax import lax
from jax.sharding import PartitionSpec as P

VARS_GENE = 4
NEED = 2
PAD_ROWS = 8


def split3(x):
    hi = lax.reduce_precision(x, exponent_bits=8, mantissa_bits=7)
    rest = x - hi
    mid = lax.reduce_precision(rest, exponent_bits=8, mantissa_bits=7)
    lo = rest - mid
    return hi.astype(jnp.bfloat16), mid.astype(jnp.bfloat16), lo.astype(jnp.bfloat16)


def batched_tile_dot(lhs, tiles):
    cols = lhs.shape[1]
    parts = jnp.concatenate(split3(lhs), axis=1)
    prod = lax.dot_general(
        parts, tiles, (((2,), (2,)), ((0,), (0,))), preferred_element_type=jnp.float32
    )
    return (prod[:, :cols] + prod[:, cols:2 * cols]) + prod[:, 2 * cols:]


def local(genotypes, variance_comp, grm_tiles, tile_rows, tile_cols, tile_live):
    cols_here, rows_here = genotypes.shape
    tile_size = grm_tiles.shape[1]
    slot_count = grm_tiles.shape[0]
    row_tiles = rows_here // tile_size
    off_count = slot_count - row_tiles
    me = lax.axis_index("ind")
    peers = lax.axis_size("ind")
    v = lax.axis_index("var")
    nvar = lax.axis_size("var")
    ncol = cols_here * nvar
    genes = ncol // VARS_GENE
    total_ind = peers * rows_here
    tau0 = variance_comp[0]
    tau1 = variance_comp[1]
    live = tile_live[0]

    eye = jnp.arange(tile_size)[:, None] == jnp.arange(tile_size)[None, :]
    diag_values = jnp.sum(
        jnp.where(eye[None], grm_tiles[:row_tiles].astype(jnp.float32), 0.0), axis=2
    )
    precond = (tau0 + tau1 * diag_values)[:, None, :]
    off_rows = tile_rows[row_tiles:]
    off_cols = tile_cols[row_tiles:]
    live_mask = (jnp.arange(row_tiles, slot_count, dtype=jnp.int32) < live).astype(jnp.float32)
    weight = (off_rows[:, None] == jnp.arange(row_tiles, dtype=jnp.int32)[None, :]).astype(jnp.float32)
    weight = weight * live_mask[:, None]
    position = off_cols // row_tiles * NEED + (off_cols % row_tiles - me) % row_tiles
    position = jnp.clip(position, 0, peers * NEED - 1)

    def to_tiles(x):
        return jnp.transpose(x.reshape(cols_here, row_tiles, tile_size), (1, 0, 2))

    def from_tiles(x):
        return jnp.transpose(x, (1, 0, 2)).reshape(cols_here, rows_here)

    def exchange(x, extra):
        rolled = jnp.stack([jnp.roll(x, -t, axis=0) for t in range(NEED)], axis=1)
        rolled = rolled.reshape(row_tiles, NEED * cols_here, tile_size)
        pieces = jnp.tile(rolled, (peers // row_tiles, 1, 1))
        flat = extra.reshape(-1)
        flat = jnp.pad(flat, (0, PAD_ROWS * tile_size - flat.shape[0]))
        side = jnp.broadcast_to(flat.reshape(1, PAD_ROWS, tile_size), (peers, PAD_ROWS, tile_size))
        pieces = jnp.concatenate([pieces, side], axis=1)
        arrived = lax.all_to_all(pieces, "ind", split_axis=0, concat_axis=0, tiled=True)
        tiles_in = arrived[:, :NEED * cols_here].reshape(peers * NEED, cols_here, tile_size)
        sums = jnp.sum(arrived[:, NEED * cols_here:].reshape(peers, -1)[:, :extra.size], axis=0)
        return tiles_in, sums.reshape(extra.shape)

    def kprod(x, tiles_in):
        picked = jnp.stack([lax.dynamic_index_in_dim(tiles_in, position[s], 0, keepdims=False)
                            for s in range(off_count)])
        prod = batched_tile_dot(jnp.concatenate([x, picked], axis=0), grm_tiles)
        far = prod[row_tiles:]
        return prod[:row_tiles] + jnp.sum(weight[:, :, None, None] * far[:, None], axis=0)

    def colsum(x):
        return jnp.sum(x, axis=(0, 2))

    geno_all = lax.all_gather(genotypes, "var", axis=0, tiled=True)
    first = v * cols_here
    a_out = first // genes
    g0 = first % genes
    geno_sub = jnp.stack(
        [to_tiles(lax.dynamic_slice_in_dim(geno_all, a * genes + g0, cols_here, 0))
         for a in range(VARS_GENE)]
    )

    g = to_tiles(genotypes)
    z0 = g / precond
    tiles0, sums0 = exchange(z0, colsum(g * z0)[None])
    rz0 = sums0[0]
    kz0 = kprod(z0, tiles0)
    image0 = tau0 * z0 + tau1 * kz0
    w = image0 / precond
    p0_local = jnp.sum(geno_sub * z0[None], axis=(1, 3))
    extra1 = jnp.concatenate([colsum(z0 * image0)[None], p0_local], axis=0)
    tiles1, sums1 = exchange(w, extra1)
    dad0 = sums1[0]
    p0 = sums1[1:]
    alpha0 = rz0 / dad0
    resid1 = g - alpha0[None, :, None] * image0
    z1 = resid1 / precond
    kw = kprod(w, tiles1)
    kz1 = kz0 - alpha0[None, :, None] * kw
    az1 = tau0 * z1 + tau1 * kz1
    red_local = jnp.concatenate(
        [colsum(resid1 * z1)[None], colsum(z1 * az1)[None],
         colsum(z1 * image0 + z0 * az1)[None], jnp.sum(geno_sub * z1[None], axis=(1, 3))],
        axis=0,
    )
    red = jnp.sum(lax.all_gather(red_local, "ind", axis=0, tiled=False), axis=0)
    rz1 = red[0]
    beta = rz1 / rz0
    dad1 = red[1] + beta * (red[2] + beta * dad0)
    alpha1 = rz1 / dad1
    dir1 = z1 + beta[None, :, None] * z0
    solution = alpha0[None, :, None] * z0 + alpha1[None, :, None] * dir1
    p1 = red[3:]
    gram_part = alpha0[None] * p0 + alpha1[None] * (p1 + beta[None] * p0)
    gathered = lax.all_gather(gram_part, "var", axis=0, tiled=False)
    full = jnp.transpose(gathered, (1, 0, 2)).reshape(VARS_GENE, ncol)
    gram_cols = lax.dynamic_index_in_dim(full, a_out, 0, keepdims=False)
    gram_cols = lax.dynamic_slice_in_dim(gram_cols.reshape(VARS_GENE, genes), g0, cols_here, 1)
    gene_gram = jnp.transpose(gram_cols) / total_ind
    return (from_tiles(solution), gene_gram)


def solution(mesh):
    placed = (P("var", "ind"), P(), P("ind", None, None), P("ind"), P("ind"), P("ind"))
    return jax.shard_map(
        local,
        mesh=mesh,
        in_specs=placed,
        out_specs=(P("var", "ind"), P("var", None)),
        check_vma=False,
    )
```

```python
import jax
import jax.numpy as jnp
from jax import lax
from jax.sharding import PartitionSpec as P

VARS_GENE = 4
NEED = 2
PAD_ROWS = 8
CHUNKS = 2


def split3(x):
    hi = lax.reduce_precision(x, exponent_bits=8, mantissa_bits=7)
    rest = x - hi
    mid = lax.reduce_precision(rest, exponent_bits=8, mantissa_bits=7)
    lo = rest - mid
    return hi.astype(jnp.bfloat16), mid.astype(jnp.bfloat16), lo.astype(jnp.bfloat16)


def batched_tile_dot(lhs, tiles):
    cols = lhs.shape[1]
    parts = jnp.concatenate(split3(lhs), axis=1)
    prod = lax.dot_general(
        parts, tiles, (((2,), (2,)), ((0,), (0,))), preferred_element_type=jnp.float32
    )
    return (prod[:, :cols] + prod[:, cols:2 * cols]) + prod[:, 2 * cols:]


def local(genotypes, variance_comp, grm_tiles, tile_rows, tile_cols, tile_live):
    cols_here, rows_here = genotypes.shape
    tile_size = grm_tiles.shape[1]
    slot_count = grm_tiles.shape[0]
    row_tiles = rows_here // tile_size
    off_count = slot_count - row_tiles
    me = lax.axis_index("ind")
    peers = lax.axis_size("ind")
    v = lax.axis_index("var")
    nvar = lax.axis_size("var")
    ncol = cols_here * nvar
    genes = ncol // VARS_GENE
    total_ind = peers * rows_here
    tau0 = variance_comp[0]
    tau1 = variance_comp[1]
    live = tile_live[0]

    eye = jnp.arange(tile_size)[:, None] == jnp.arange(tile_size)[None, :]
    diag_values = jnp.sum(
        jnp.where(eye[None], grm_tiles[:row_tiles].astype(jnp.float32), 0.0), axis=2
    )
    precond = (tau0 + tau1 * diag_values)[:, None, :]
    off_rows = tile_rows[row_tiles:]
    off_cols = tile_cols[row_tiles:]
    live_mask = (jnp.arange(row_tiles, slot_count, dtype=jnp.int32) < live).astype(jnp.float32)
    weight = (off_rows[:, None] == jnp.arange(row_tiles, dtype=jnp.int32)[None, :]).astype(jnp.float32)
    weight = weight * live_mask[:, None]
    position = off_cols // row_tiles * NEED + (off_cols % row_tiles - me) % row_tiles
    position = jnp.clip(position, 0, peers * NEED - 1)

    def to_tiles(x):
        return jnp.transpose(x.reshape(cols_here, row_tiles, tile_size), (1, 0, 2))

    def from_tiles(x):
        return jnp.transpose(x, (1, 0, 2)).reshape(cols_here, rows_here)

    def exchange(x, extra):
        rolled = jnp.stack([jnp.roll(x, -t, axis=0) for t in range(NEED)], axis=1)
        width = x.shape[1]
        rolled = rolled.reshape(row_tiles, NEED * width, tile_size)
        pieces = jnp.tile(rolled, (peers // row_tiles, 1, 1))
        flat = extra.reshape(-1)
        flat = jnp.pad(flat, (0, PAD_ROWS * tile_size - flat.shape[0]))
        side = jnp.broadcast_to(flat.reshape(1, PAD_ROWS, tile_size), (peers, PAD_ROWS, tile_size))
        pieces = jnp.concatenate([pieces, side], axis=1)
        arrived = lax.all_to_all(pieces, "ind", split_axis=0, concat_axis=0, tiled=True)
        tiles_in = arrived[:, :NEED * width].reshape(peers * NEED, width, tile_size)
        sums = jnp.sum(arrived[:, NEED * width:].reshape(peers, -1)[:, :extra.size], axis=0)
        return tiles_in, sums.reshape(extra.shape)

    def kprod(x, tiles_in):
        picked = jnp.stack([lax.dynamic_index_in_dim(tiles_in, position[s], 0, keepdims=False)
                            for s in range(off_count)])
        prod = batched_tile_dot(jnp.concatenate([x, picked], axis=0), grm_tiles)
        far = prod[row_tiles:]
        return prod[:row_tiles] + jnp.sum(weight[:, :, None, None] * far[:, None], axis=0)

    def colsum(x):
        return jnp.sum(x, axis=(0, 2))

    geno_all = lax.all_gather(genotypes, "var", axis=0, tiled=True)
    first = v * cols_here
    a_out = first // genes
    g0 = first % genes
    geno_sub = jnp.stack(
        [to_tiles(lax.dynamic_slice_in_dim(geno_all, a * genes + g0, cols_here, 0))
         for a in range(VARS_GENE)]
    )

    def reduce_ind(x):
        spread = jnp.broadcast_to(x[None], (peers,) + x.shape)
        return jnp.sum(lax.all_to_all(spread, "ind", split_axis=0, concat_axis=0, tiled=True), axis=0)

    def chunk(g, geno_sub):
        z0 = g / precond
        tiles0, sums0 = exchange(z0, colsum(g * z0)[None])
        rz0 = sums0[0]
        kz0 = kprod(z0, tiles0)
        image0 = tau0 * z0 + tau1 * kz0
        w = image0 / precond
        p0_local = jnp.sum(geno_sub * z0[None], axis=(1, 3))
        extra1 = jnp.concatenate([colsum(z0 * image0)[None], p0_local], axis=0)
        tiles1, sums1 = exchange(w, extra1)
        dad0 = sums1[0]
        p0 = sums1[1:]
        alpha0 = rz0 / dad0
        resid1 = g - alpha0[None, :, None] * image0
        z1 = resid1 / precond
        kw = kprod(w, tiles1)
        kz1 = kz0 - alpha0[None, :, None] * kw
        az1 = tau0 * z1 + tau1 * kz1
        red_local = jnp.concatenate(
            [colsum(resid1 * z1)[None], colsum(z1 * az1)[None],
             colsum(z1 * image0 + z0 * az1)[None], jnp.sum(geno_sub * z1[None], axis=(1, 3))],
            axis=0,
        )
        red = reduce_ind(red_local)
        rz1 = red[0]
        beta = rz1 / rz0
        dad1 = red[1] + beta * (red[2] + beta * dad0)
        alpha1 = rz1 / dad1
        dir1 = z1 + beta[None, :, None] * z0
        sol = alpha0[None, :, None] * z0 + alpha1[None, :, None] * dir1
        p1 = red[3:]
        part = alpha0[None] * p0 + alpha1[None] * (p1 + beta[None] * p0)
        return sol, part

    g_all = to_tiles(genotypes)
    width = cols_here // CHUNKS
    outs = [chunk(g_all[:, k * width:(k + 1) * width], geno_sub[:, :, k * width:(k + 1) * width])
            for k in range(CHUNKS)]
    solution = jnp.concatenate([o[0] for o in outs], axis=1)
    gram_part = jnp.concatenate([o[1] for o in outs], axis=1)
    gathered = lax.all_gather(gram_part, "var", axis=0, tiled=False)
    full = jnp.transpose(gathered, (1, 0, 2)).reshape(VARS_GENE, ncol)
    gram_cols = lax.dynamic_index_in_dim(full, a_out, 0, keepdims=False)
    gram_cols = lax.dynamic_slice_in_dim(gram_cols.reshape(VARS_GENE, genes), g0, cols_here, 1)
    gene_gram = jnp.transpose(gram_cols) / total_ind
    return (from_tiles(solution), gene_gram)


def solution(mesh):
    placed = (P("var", "ind"), P(), P("ind", None, None), P("ind"), P("ind"), P("ind"))
    return jax.shard_map(
        local,
        mesh=mesh,
        in_specs=placed,
        out_specs=(P("var", "ind"), P("var", None)),
        check_vma=False,
    )
```

```python
import jax
import jax.numpy as jnp
from jax import lax
from jax.sharding import PartitionSpec as P

VARS_GENE = 4
NEED = 2
PAD_ROWS = 8
CHUNKS = 1


def split3(x):
    hi = lax.reduce_precision(x, exponent_bits=8, mantissa_bits=7)
    rest = x - hi
    mid = lax.reduce_precision(rest, exponent_bits=8, mantissa_bits=7)
    lo = rest - mid
    return hi.astype(jnp.bfloat16), mid.astype(jnp.bfloat16), lo.astype(jnp.bfloat16)


def batched_tile_dot(lhs, tiles):
    cols = lhs.shape[1]
    parts = jnp.concatenate(split3(lhs), axis=1)
    prod = lax.dot_general(
        parts, tiles, (((2,), (2,)), ((0,), (0,))), preferred_element_type=jnp.float32
    )
    return (prod[:, :cols] + prod[:, cols:2 * cols]) + prod[:, 2 * cols:]


def local(genotypes, variance_comp, grm_tiles, tile_rows, tile_cols, tile_live):
    cols_here, rows_here = genotypes.shape
    tile_size = grm_tiles.shape[1]
    slot_count = grm_tiles.shape[0]
    row_tiles = rows_here // tile_size
    off_count = slot_count - row_tiles
    me = lax.axis_index("ind")
    peers = lax.axis_size("ind")
    v = lax.axis_index("var")
    nvar = lax.axis_size("var")
    ncol = cols_here * nvar
    genes = ncol // VARS_GENE
    total_ind = peers * rows_here
    tau0 = variance_comp[0]
    tau1 = variance_comp[1]
    live = tile_live[0]

    eye = jnp.arange(tile_size)[:, None] == jnp.arange(tile_size)[None, :]
    diag_values = jnp.sum(
        jnp.where(eye[None], grm_tiles[:row_tiles].astype(jnp.float32), 0.0), axis=2
    )
    precond = (tau0 + tau1 * diag_values)[:, None, :]
    off_rows = tile_rows[row_tiles:]
    off_cols = tile_cols[row_tiles:]
    live_mask = (jnp.arange(row_tiles, slot_count, dtype=jnp.int32) < live).astype(jnp.float32)
    weight = (off_rows[:, None] == jnp.arange(row_tiles, dtype=jnp.int32)[None, :]).astype(jnp.float32)
    weight = weight * live_mask[:, None]
    position = off_cols // row_tiles * NEED + (off_cols % row_tiles - me) % row_tiles
    position = jnp.clip(position, 0, peers * NEED - 1)

    def to_tiles(x):
        return jnp.transpose(x.reshape(cols_here, row_tiles, tile_size), (1, 0, 2))

    def from_tiles(x):
        return jnp.transpose(x, (1, 0, 2)).reshape(cols_here, rows_here)

    def exchange(x, extra):
        rolled = jnp.stack([jnp.roll(x, -t, axis=0) for t in range(NEED)], axis=1)
        width = x.shape[1]
        rolled = rolled.reshape(row_tiles, NEED * width, tile_size)
        pieces = jnp.tile(rolled, (peers // row_tiles, 1, 1))
        flat = extra.reshape(-1)
        flat = jnp.pad(flat, (0, PAD_ROWS * tile_size - flat.shape[0]))
        side = jnp.broadcast_to(flat.reshape(1, PAD_ROWS, tile_size), (peers, PAD_ROWS, tile_size))
        pieces = jnp.concatenate([pieces, side], axis=1)
        arrived = lax.all_to_all(pieces, "ind", split_axis=0, concat_axis=0, tiled=True)
        tiles_in = arrived[:, :NEED * width].reshape(peers * NEED, width, tile_size)
        sums = jnp.sum(arrived[:, NEED * width:].reshape(peers, -1)[:, :extra.size], axis=0)
        return tiles_in, sums.reshape(extra.shape)

    def kprod(x, tiles_in):
        picked = jnp.stack([lax.dynamic_index_in_dim(tiles_in, position[s], 0, keepdims=False)
                            for s in range(off_count)])
        prod = batched_tile_dot(jnp.concatenate([x, picked], axis=0), grm_tiles)
        far = prod[row_tiles:]
        return prod[:row_tiles] + jnp.sum(weight[:, :, None, None] * far[:, None], axis=0)

    def colsum(x):
        return jnp.sum(x, axis=(0, 2))

    geno_all = lax.all_gather(genotypes, "var", axis=0, tiled=True)
    first = v * cols_here
    a_out = first // genes
    g0 = first % genes
    geno_sub = jnp.stack(
        [to_tiles(lax.dynamic_slice_in_dim(geno_all, a * genes + g0, cols_here, 0))
         for a in range(VARS_GENE)]
    )

    def reduce_ind(x):
        spread = jnp.broadcast_to(x[None], (peers,) + x.shape)
        return jnp.sum(lax.all_to_all(spread, "ind", split_axis=0, concat_axis=0, tiled=True), axis=0)

    def chunk(g, geno_sub):
        z0 = g / precond
        tiles0, sums0 = exchange(z0, colsum(g * z0)[None])
        rz0 = sums0[0]
        kz0 = kprod(z0, tiles0)
        image0 = tau0 * z0 + tau1 * kz0
        w = image0 / precond
        p0_local = jnp.sum(geno_sub * z0[None], axis=(1, 3))
        extra1 = jnp.concatenate([colsum(z0 * image0)[None], p0_local], axis=0)
        tiles1, sums1 = exchange(w, extra1)
        dad0 = sums1[0]
        p0 = sums1[1:]
        alpha0 = rz0 / dad0
        resid1 = g - alpha0[None, :, None] * image0
        z1 = resid1 / precond
        kw = kprod(w, tiles1)
        kz1 = kz0 - alpha0[None, :, None] * kw
        az1 = tau0 * z1 + tau1 * kz1
        red_local = jnp.concatenate(
            [colsum(resid1 * z1)[None], colsum(z1 * az1)[None],
             colsum(z1 * image0 + z0 * az1)[None], jnp.sum(geno_sub * z1[None], axis=(1, 3))],
            axis=0,
        )
        red = reduce_ind(red_local)
        rz1 = red[0]
        beta = rz1 / rz0
        dad1 = red[1] + beta * (red[2] + beta * dad0)
        alpha1 = rz1 / dad1
        dir1 = z1 + beta[None, :, None] * z0
        sol = alpha0[None, :, None] * z0 + alpha1[None, :, None] * dir1
        p1 = red[3:]
        part = alpha0[None] * p0 + alpha1[None] * (p1 + beta[None] * p0)
        return sol, part

    g_all = to_tiles(genotypes)
    width = cols_here // CHUNKS
    outs = [chunk(g_all[:, k * width:(k + 1) * width], geno_sub[:, :, k * width:(k + 1) * width])
            for k in range(CHUNKS)]
    solution = jnp.concatenate([o[0] for o in outs], axis=1)
    gram_part = jnp.concatenate([o[1] for o in outs], axis=1)
    gathered = lax.all_gather(gram_part, "var", axis=0, tiled=False)
    full = jnp.transpose(gathered, (1, 0, 2)).reshape(VARS_GENE, ncol)
    gram_cols = lax.dynamic_index_in_dim(full, a_out, 0, keepdims=False)
    gram_cols = lax.dynamic_slice_in_dim(gram_cols.reshape(VARS_GENE, genes), g0, cols_here, 1)
    gene_gram = jnp.transpose(gram_cols) / total_ind
    return (from_tiles(solution), gene_gram)


def solution(mesh):
    placed = (P("var", "ind"), P(), P("ind", None, None), P("ind"), P("ind"), P("ind"))
    return jax.shard_map(
        local,
        mesh=mesh,
        in_specs=placed,
        out_specs=(P("var", "ind"), P("var", None)),
        check_vma=False,
    )
```

```python
import jax
import jax.numpy as jnp
from jax import lax
from jax.sharding import PartitionSpec as P

VARS_GENE = 4
NEED = 2
PAD_ROWS = 8
CHUNKS = 1


def split3(x):
    hi = lax.reduce_precision(x, exponent_bits=8, mantissa_bits=7)
    rest = x - hi
    mid = lax.reduce_precision(rest, exponent_bits=8, mantissa_bits=7)
    lo = rest - mid
    return hi.astype(jnp.bfloat16), mid.astype(jnp.bfloat16), lo.astype(jnp.bfloat16)


def batched_tile_dot(lhs, tiles):
    cols = lhs.shape[1]
    parts = jnp.concatenate(split3(lhs), axis=1)
    prod = lax.dot_general(
        parts, tiles, (((2,), (2,)), ((0,), (0,))), preferred_element_type=jnp.float32
    )
    return (prod[:, :cols] + prod[:, cols:2 * cols]) + prod[:, 2 * cols:]


def local(genotypes, variance_comp, grm_tiles, tile_rows, tile_cols, tile_live):
    cols_here, rows_here = genotypes.shape
    tile_size = grm_tiles.shape[1]
    slot_count = grm_tiles.shape[0]
    row_tiles = rows_here // tile_size
    off_count = slot_count - row_tiles
    me = lax.axis_index("ind")
    peers = lax.axis_size("ind")
    v = lax.axis_index("var")
    nvar = lax.axis_size("var")
    ncol = cols_here * nvar
    genes = ncol // VARS_GENE
    total_ind = peers * rows_here
    tau0 = variance_comp[0]
    tau1 = variance_comp[1]
    live = tile_live[0]

    eye = jnp.arange(tile_size)[:, None] == jnp.arange(tile_size)[None, :]
    diag_values = jnp.sum(
        jnp.where(eye[None], grm_tiles[:row_tiles].astype(jnp.float32), 0.0), axis=2
    )
    precond = (tau0 + tau1 * diag_values)[:, None, :]
    off_rows = tile_rows[row_tiles:]
    off_cols = tile_cols[row_tiles:]
    live_mask = (jnp.arange(row_tiles, slot_count, dtype=jnp.int32) < live).astype(jnp.float32)
    weight = (off_rows[:, None] == jnp.arange(row_tiles, dtype=jnp.int32)[None, :]).astype(jnp.float32)
    weight = weight * live_mask[:, None]
    position = off_cols // row_tiles * NEED + (off_cols % row_tiles - me) % row_tiles
    position = jnp.clip(position, 0, peers * NEED - 1)

    def to_tiles(x):
        return jnp.transpose(x.reshape(cols_here, row_tiles, tile_size), (1, 0, 2))

    def from_tiles(x):
        return jnp.transpose(x, (1, 0, 2)).reshape(cols_here, rows_here)

    def exchange(x, extra):
        rolled = jnp.stack([jnp.roll(x, -t, axis=0) for t in range(NEED)], axis=1)
        width = x.shape[1]
        rolled = rolled.reshape(row_tiles, NEED * width, tile_size)
        pieces = jnp.tile(rolled, (peers // row_tiles, 1, 1))
        if extra is not None:
            flat = extra.reshape(-1)
            flat = jnp.pad(flat, (0, PAD_ROWS * tile_size - flat.shape[0]))
            side = jnp.broadcast_to(flat.reshape(1, PAD_ROWS, tile_size), (peers, PAD_ROWS, tile_size))
            pieces = jnp.concatenate([pieces, side], axis=1)
        arrived = lax.all_to_all(pieces, "ind", split_axis=0, concat_axis=0, tiled=True)
        sums = None
        if extra is not None:
            sums = jnp.sum(arrived[:, NEED * width:].reshape(peers, -1)[:, :extra.size], axis=0)
            sums = sums.reshape(extra.shape)
        return arrived, sums

    def kprod(x, arrived):
        width = x.shape[1]
        picked = jnp.stack([
            lax.dynamic_slice(arrived, (position[s] // NEED, position[s] % NEED * width, 0),
                              (1, width, tile_size))[0]
            for s in range(off_count)])
        prod = batched_tile_dot(jnp.concatenate([x, picked], axis=0), grm_tiles)
        far = prod[row_tiles:]
        return prod[:row_tiles] + jnp.sum(weight[:, :, None, None] * far[:, None], axis=0)

    def colsum(x):
        return jnp.sum(x, axis=(0, 2))

    geno_all = lax.all_gather(genotypes, "var", axis=0, tiled=True)
    first = v * cols_here
    a_out = first // genes
    g0 = first % genes
    geno_sub = jnp.stack(
        [to_tiles(lax.dynamic_slice_in_dim(geno_all, a * genes + g0, cols_here, 0))
         for a in range(VARS_GENE)]
    )

    def chunk(g, geno_sub):
        z0 = g / precond
        tiles0, _ = exchange(z0, None)
        kz0 = kprod(z0, tiles0)
        image0 = tau0 * z0 + tau1 * kz0
        w = image0 / precond
        p0_local = jnp.sum(geno_sub * z0[None], axis=(1, 3))
        extra1 = jnp.concatenate([colsum(g * z0)[None], colsum(z0 * image0)[None], p0_local], axis=0)
        tiles1, sums1 = exchange(w, extra1)
        rz0 = sums1[0]
        dad0 = sums1[1]
        p0 = sums1[2:]
        alpha0 = rz0 / dad0
        resid1 = g - alpha0[None, :, None] * image0
        z1 = resid1 / precond
        kw = kprod(w, tiles1)
        kz1 = kz0 - alpha0[None, :, None] * kw
        az1 = tau0 * z1 + tau1 * kz1
        red_local = jnp.concatenate(
            [colsum(resid1 * z1)[None], colsum(z1 * az1)[None],
             colsum(z1 * image0 + z0 * az1)[None], jnp.sum(geno_sub * z1[None], axis=(1, 3))],
            axis=0,
        )
        lead = (me == 0).astype(jnp.float32)
        payload = jnp.concatenate(
            [red_local, lead * rz0[None], lead * dad0[None], lead * p0], axis=0)
        spread = jnp.broadcast_to(payload[None], (peers * nvar,) + payload.shape)
        got = lax.all_to_all(spread, ("ind", "var"), split_axis=0, concat_axis=0, tiled=True)
        tot = jnp.sum(got.reshape((peers, nvar) + payload.shape), axis=0)
        nv = VARS_GENE
        rz1_all = tot[:, 0]
        rz0_all = tot[:, 3 + nv]
        dad0_all = tot[:, 4 + nv]
        p0_all = tot[:, 5 + nv:]
        p1_all = tot[:, 3:3 + nv]
        alpha0_all = rz0_all / dad0_all
        beta_all = rz1_all / rz0_all
        dad1_all = tot[:, 1] + beta_all * (tot[:, 2] + beta_all * dad0_all)
        alpha1_all = rz1_all / dad1_all
        mine = lambda t: lax.dynamic_index_in_dim(t, v, 0, keepdims=False)
        beta = mine(beta_all)
        alpha1 = mine(alpha1_all)
        dir1 = z1 + beta[None, :, None] * z0
        sol = alpha0[None, :, None] * z0 + alpha1[None, :, None] * dir1
        part = alpha0_all[:, None] * p0_all + alpha1_all[:, None] * (p1_all + beta_all[:, None] * p0_all)
        return sol, part

    g_all = to_tiles(genotypes)
    width = cols_here // CHUNKS
    outs = [chunk(g_all[:, k * width:(k + 1) * width], geno_sub[:, :, k * width:(k + 1) * width])
            for k in range(CHUNKS)]
    solution = jnp.concatenate([o[0] for o in outs], axis=1)
    gram_part = jnp.concatenate([o[1] for o in outs], axis=2)
    full = jnp.transpose(gram_part, (1, 0, 2)).reshape(VARS_GENE, ncol)
    gram_cols = lax.dynamic_index_in_dim(full, a_out, 0, keepdims=False)
    gram_cols = lax.dynamic_slice_in_dim(gram_cols.reshape(VARS_GENE, genes), g0, cols_here, 1)
    gene_gram = jnp.transpose(gram_cols) / total_ind
    return (from_tiles(solution), gene_gram)


def solution(mesh):
    placed = (P("var", "ind"), P(), P("ind", None, None), P("ind"), P("ind"), P("ind"))
    return jax.shard_map(
        local,
        mesh=mesh,
        in_specs=placed,
        out_specs=(P("var", "ind"), P("var", None)),
        check_vma=False,
    )
```

```python
import jax
import jax.numpy as jnp
from jax import lax
from jax.sharding import PartitionSpec as P

VARS_GENE = 4
NEED = 2
PAD_ROWS = 8
CHUNKS = 1


def split3(x):
    hi = lax.reduce_precision(x, exponent_bits=8, mantissa_bits=7)
    rest = x - hi
    mid = lax.reduce_precision(rest, exponent_bits=8, mantissa_bits=7)
    lo = rest - mid
    return hi.astype(jnp.bfloat16), mid.astype(jnp.bfloat16), lo.astype(jnp.bfloat16)


def batched_tile_dot(lhs, tiles):
    cols = lhs.shape[1]
    parts = jnp.concatenate(split3(lhs), axis=1)
    prod = lax.dot_general(
        parts, tiles, (((2,), (2,)), ((0,), (0,))), preferred_element_type=jnp.float32
    )
    return (prod[:, :cols] + prod[:, cols:2 * cols]) + prod[:, 2 * cols:]


def local(genotypes, variance_comp, grm_tiles, tile_rows, tile_cols, tile_live):
    cols_here, rows_here = genotypes.shape
    tile_size = grm_tiles.shape[1]
    slot_count = grm_tiles.shape[0]
    row_tiles = rows_here // tile_size
    off_count = slot_count - row_tiles
    me = lax.axis_index("ind")
    peers = lax.axis_size("ind")
    v = lax.axis_index("var")
    nvar = lax.axis_size("var")
    ncol = cols_here * nvar
    genes = ncol // VARS_GENE
    total_ind = peers * rows_here
    tau0 = variance_comp[0]
    tau1 = variance_comp[1]
    live = tile_live[0]

    eye = jnp.arange(tile_size)[:, None] == jnp.arange(tile_size)[None, :]
    diag_values = jnp.sum(
        jnp.where(eye[None], grm_tiles[:row_tiles].astype(jnp.float32), 0.0), axis=2
    )
    precond = (tau0 + tau1 * diag_values)[:, None, :]
    off_rows = tile_rows[row_tiles:]
    off_cols = tile_cols[row_tiles:]
    live_mask = (jnp.arange(row_tiles, slot_count, dtype=jnp.int32) < live).astype(jnp.float32)
    weight = (off_rows[:, None] == jnp.arange(row_tiles, dtype=jnp.int32)[None, :]).astype(jnp.float32)
    weight = weight * live_mask[:, None]
    position = off_cols // row_tiles * NEED + (off_cols % row_tiles - me) % row_tiles
    position = jnp.clip(position, 0, peers * NEED - 1)

    def to_tiles(x):
        return jnp.transpose(x.reshape(cols_here, row_tiles, tile_size), (1, 0, 2))

    def from_tiles(x):
        return jnp.transpose(x, (1, 0, 2)).reshape(cols_here, rows_here)

    def exchange(x, extra):
        rolled = jnp.stack([jnp.roll(x, -t, axis=0) for t in range(NEED)], axis=1)
        width = x.shape[1]
        rolled = rolled.reshape(row_tiles, NEED * width, tile_size)
        pieces = jnp.tile(rolled, (peers // row_tiles, 1, 1))
        if extra is not None:
            flat = extra.reshape(-1)
            flat = jnp.pad(flat, (0, PAD_ROWS * tile_size - flat.shape[0]))
            side = jnp.broadcast_to(flat.reshape(1, PAD_ROWS, tile_size), (peers, PAD_ROWS, tile_size))
            pieces = jnp.concatenate([pieces, side], axis=1)
        arrived = lax.all_to_all(pieces, "ind", split_axis=0, concat_axis=0, tiled=True)
        if extra is None:
            return arrived.reshape(peers * NEED, width, tile_size), None
        tiles_in = arrived[:, :NEED * width].reshape(peers * NEED, width, tile_size)
        sums = jnp.sum(arrived[:, NEED * width:].reshape(peers, -1)[:, :extra.size], axis=0)
        return tiles_in, sums.reshape(extra.shape)

    def kprod(x, arrived):
        width = x.shape[1]
        picked = jnp.stack([lax.dynamic_index_in_dim(arrived, position[s], 0, keepdims=False)
                            for s in range(off_count)])
        prod = batched_tile_dot(jnp.concatenate([x, picked], axis=0), grm_tiles)
        far = prod[row_tiles:]
        return prod[:row_tiles] + jnp.sum(weight[:, :, None, None] * far[:, None], axis=0)

    def colsum(x):
        return jnp.sum(x, axis=(0, 2))

    geno_all = lax.all_gather(genotypes, "var", axis=0, tiled=True)
    first = v * cols_here
    a_out = first // genes
    g0 = first % genes
    geno_sub = jnp.stack(
        [to_tiles(lax.dynamic_slice_in_dim(geno_all, a * genes + g0, cols_here, 0))
         for a in range(VARS_GENE)]
    )

    def chunk(g, geno_sub):
        z0 = g / precond
        tiles0, _ = exchange(z0, None)
        kz0 = kprod(z0, tiles0)
        image0 = tau0 * z0 + tau1 * kz0
        w = image0 / precond
        p0_local = jnp.sum(geno_sub * z0[None], axis=(1, 3))
        extra1 = jnp.concatenate([colsum(g * z0)[None], colsum(z0 * image0)[None], p0_local], axis=0)
        tiles1, sums1 = exchange(w, extra1)
        rz0 = sums1[0]
        dad0 = sums1[1]
        p0 = sums1[2:]
        alpha0 = rz0 / dad0
        resid1 = g - alpha0[None, :, None] * image0
        z1 = resid1 / precond
        kw = kprod(w, tiles1)
        kz1 = kz0 - alpha0[None, :, None] * kw
        az1 = tau0 * z1 + tau1 * kz1
        red_local = jnp.concatenate(
            [colsum(resid1 * z1)[None], colsum(z1 * az1)[None],
             colsum(z1 * image0 + z0 * az1)[None], jnp.sum(geno_sub * z1[None], axis=(1, 3))],
            axis=0,
        )
        lead = (me == 0).astype(jnp.float32)
        payload = jnp.concatenate(
            [red_local, lead * rz0[None], lead * dad0[None], lead * p0], axis=0)
        spread = jnp.broadcast_to(payload[None], (peers * nvar,) + payload.shape)
        got = lax.all_to_all(spread, ("ind", "var"), split_axis=0, concat_axis=0, tiled=True)
        tot = jnp.sum(got.reshape((peers, nvar) + payload.shape), axis=0)
        nv = VARS_GENE
        rz1_all = tot[:, 0]
        rz0_all = tot[:, 3 + nv]
        dad0_all = tot[:, 4 + nv]
        p0_all = tot[:, 5 + nv:]
        p1_all = tot[:, 3:3 + nv]
        alpha0_all = rz0_all / dad0_all
        beta_all = rz1_all / rz0_all
        dad1_all = tot[:, 1] + beta_all * (tot[:, 2] + beta_all * dad0_all)
        alpha1_all = rz1_all / dad1_all
        mine = lambda t: lax.dynamic_index_in_dim(t, v, 0, keepdims=False)
        beta = mine(beta_all)
        alpha1 = mine(alpha1_all)
        dir1 = z1 + beta[None, :, None] * z0
        sol = alpha0[None, :, None] * z0 + alpha1[None, :, None] * dir1
        part = alpha0_all[:, None] * p0_all + alpha1_all[:, None] * (p1_all + beta_all[:, None] * p0_all)
        return sol, part

    g_all = to_tiles(genotypes)
    width = cols_here // CHUNKS
    outs = [chunk(g_all[:, k * width:(k + 1) * width], geno_sub[:, :, k * width:(k + 1) * width])
            for k in range(CHUNKS)]
    solution = jnp.concatenate([o[0] for o in outs], axis=1)
    gram_part = jnp.concatenate([o[1] for o in outs], axis=2)
    full = jnp.transpose(gram_part, (1, 0, 2)).reshape(VARS_GENE, ncol)
    gram_cols = lax.dynamic_index_in_dim(full, a_out, 0, keepdims=False)
    gram_cols = lax.dynamic_slice_in_dim(gram_cols.reshape(VARS_GENE, genes), g0, cols_here, 1)
    gene_gram = jnp.transpose(gram_cols) / total_ind
    return (from_tiles(solution), gene_gram)


def solution(mesh):
    placed = (P("var", "ind"), P(), P("ind", None, None), P("ind"), P("ind"), P("ind"))
    return jax.shard_map(
        local,
        mesh=mesh,
        in_specs=placed,
        out_specs=(P("var", "ind"), P("var", None)),
        check_vma=False,
    )
```

```python
import jax
import jax.numpy as jnp
from jax import lax
from jax.sharding import PartitionSpec as P

VARS_GENE = 4
NEED = 2
PAD_ROWS = 8
CHUNKS = 1


def split3(x):
    hi = lax.reduce_precision(x, exponent_bits=8, mantissa_bits=7)
    rest = x - hi
    mid = lax.reduce_precision(rest, exponent_bits=8, mantissa_bits=7)
    lo = rest - mid
    return hi.astype(jnp.bfloat16), mid.astype(jnp.bfloat16), lo.astype(jnp.bfloat16)


def batched_tile_dot(lhs, tiles):
    cols = lhs.shape[1]
    parts = jnp.concatenate(split3(lhs), axis=1)
    prod = lax.dot_general(
        parts, tiles, (((2,), (2,)), ((0,), (0,))), preferred_element_type=jnp.float32
    )
    return (prod[:, :cols] + prod[:, cols:2 * cols]) + prod[:, 2 * cols:]


def local(genotypes, variance_comp, grm_tiles, tile_rows, tile_cols, tile_live):
    cols_here, rows_here = genotypes.shape
    tile_size = grm_tiles.shape[1]
    slot_count = grm_tiles.shape[0]
    row_tiles = rows_here // tile_size
    off_count = slot_count - row_tiles
    me = lax.axis_index("ind")
    peers = lax.axis_size("ind")
    v = lax.axis_index("var")
    nvar = lax.axis_size("var")
    ncol = cols_here * nvar
    genes = ncol // VARS_GENE
    total_ind = peers * rows_here
    tau0 = variance_comp[0]
    tau1 = variance_comp[1]
    live = tile_live[0]

    eye = jnp.arange(tile_size)[:, None] == jnp.arange(tile_size)[None, :]
    diag_values = jnp.sum(
        jnp.where(eye[None], grm_tiles[:row_tiles].astype(jnp.float32), 0.0), axis=2
    )
    precond = (tau0 + tau1 * diag_values)[:, None, :]
    off_rows = tile_rows[row_tiles:]
    off_cols = tile_cols[row_tiles:]
    live_mask = (jnp.arange(row_tiles, slot_count, dtype=jnp.int32) < live).astype(jnp.float32)
    weight = (off_rows[:, None] == jnp.arange(row_tiles, dtype=jnp.int32)[None, :]).astype(jnp.float32)
    weight = weight * live_mask[:, None]
    position = off_cols // row_tiles * NEED + (off_cols % row_tiles - me) % row_tiles
    position = jnp.clip(position, 0, peers * NEED - 1)

    def to_tiles(x):
        return jnp.transpose(x.reshape(cols_here, row_tiles, tile_size), (1, 0, 2))

    def from_tiles(x):
        return jnp.transpose(x, (1, 0, 2)).reshape(cols_here, rows_here)

    def exchange(x, extra):
        rolled = jnp.stack([jnp.roll(x, -t, axis=0) for t in range(NEED)], axis=1)
        width = x.shape[1]
        rolled = rolled.reshape(row_tiles, NEED * width, tile_size)
        pieces = jnp.tile(rolled, (peers // row_tiles, 1, 1))
        if extra is not None:
            flat = extra.reshape(-1)
            flat = jnp.pad(flat, (0, PAD_ROWS * tile_size - flat.shape[0]))
            side = jnp.broadcast_to(flat.reshape(1, PAD_ROWS, tile_size), (peers, PAD_ROWS, tile_size))
            pieces = jnp.concatenate([pieces, side], axis=1)
        arrived = lax.all_to_all(pieces, "ind", split_axis=0, concat_axis=0, tiled=True)
        if extra is None:
            return arrived.reshape(peers * NEED, width, tile_size), None
        tiles_in = arrived[:, :NEED * width].reshape(peers * NEED, width, tile_size)
        sums = jnp.sum(arrived[:, NEED * width:].reshape(peers, -1)[:, :extra.size], axis=0)
        return tiles_in, sums.reshape(extra.shape)

    def kprod(x, arrived):
        width = x.shape[1]
        picked = jnp.stack([lax.dynamic_index_in_dim(arrived, position[s], 0, keepdims=False)
                            for s in range(off_count)])
        prod = batched_tile_dot(jnp.concatenate([x, picked], axis=0), grm_tiles)
        far = prod[row_tiles:]
        return prod[:row_tiles] + jnp.sum(weight[:, :, None, None] * far[:, None], axis=0)

    def colsum(x):
        return jnp.sum(x, axis=(0, 2))

    geno_all = lax.all_gather(genotypes, "var", axis=0, tiled=True)
    first = v * cols_here
    a_out = first // genes
    g0 = first % genes
    geno_sub = jnp.stack(
        [to_tiles(lax.dynamic_slice_in_dim(geno_all, a * genes + g0, cols_here, 0))
         for a in range(VARS_GENE)]
    )

    def chunk(g, geno_sub):
        z0 = g / precond
        tiles0, sums0 = exchange(z0, colsum(g * z0)[None])
        rz0 = sums0[0]
        kz0 = kprod(z0, tiles0)
        image0 = tau0 * z0 + tau1 * kz0
        w = image0 / precond
        p0_local = jnp.sum(geno_sub * z0[None], axis=(1, 3))
        extra1 = jnp.concatenate([colsum(z0 * image0)[None], p0_local], axis=0)
        tiles1, sums1 = exchange(w, extra1)
        dad0 = sums1[0]
        p0 = sums1[1:]
        alpha0 = rz0 / dad0
        resid1 = g - alpha0[None, :, None] * image0
        z1 = resid1 / precond
        kw = kprod(w, tiles1)
        kz1 = kz0 - alpha0[None, :, None] * kw
        az1 = tau0 * z1 + tau1 * kz1
        red_local = jnp.concatenate(
            [colsum(resid1 * z1)[None], colsum(z1 * az1)[None],
             colsum(z1 * image0 + z0 * az1)[None], jnp.sum(geno_sub * z1[None], axis=(1, 3))],
            axis=0,
        )
        lead = (me == 0).astype(jnp.float32)
        payload = jnp.concatenate(
            [red_local, lead * rz0[None], lead * dad0[None], lead * p0], axis=0)
        spread = jnp.broadcast_to(payload[None], (peers * nvar,) + payload.shape)
        got = lax.all_to_all(spread, ("ind", "var"), split_axis=0, concat_axis=0, tiled=True)
        tot = jnp.sum(got.reshape((peers, nvar) + payload.shape), axis=0)
        nv = VARS_GENE
        rz1_all = tot[:, 0]
        rz0_all = tot[:, 3 + nv]
        dad0_all = tot[:, 4 + nv]
        p0_all = tot[:, 5 + nv:]
        p1_all = tot[:, 3:3 + nv]
        alpha0_all = rz0_all / dad0_all
        beta_all = rz1_all / rz0_all
        dad1_all = tot[:, 1] + beta_all * (tot[:, 2] + beta_all * dad0_all)
        alpha1_all = rz1_all / dad1_all
        mine = lambda t: lax.dynamic_index_in_dim(t, v, 0, keepdims=False)
        beta = mine(beta_all)
        alpha1 = mine(alpha1_all)
        dir1 = z1 + beta[None, :, None] * z0
        sol = alpha0[None, :, None] * z0 + alpha1[None, :, None] * dir1
        part = alpha0_all[:, None] * p0_all + alpha1_all[:, None] * (p1_all + beta_all[:, None] * p0_all)
        return sol, part

    g_all = to_tiles(genotypes)
    width = cols_here // CHUNKS
    outs = [chunk(g_all[:, k * width:(k + 1) * width], geno_sub[:, :, k * width:(k + 1) * width])
            for k in range(CHUNKS)]
    solution = jnp.concatenate([o[0] for o in outs], axis=1)
    gram_part = jnp.concatenate([o[1] for o in outs], axis=2)
    full = jnp.transpose(gram_part, (1, 0, 2)).reshape(VARS_GENE, ncol)
    gram_cols = lax.dynamic_index_in_dim(full, a_out, 0, keepdims=False)
    gram_cols = lax.dynamic_slice_in_dim(gram_cols.reshape(VARS_GENE, genes), g0, cols_here, 1)
    gene_gram = jnp.transpose(gram_cols) / total_ind
    return (from_tiles(solution), gene_gram)


def solution(mesh):
    placed = (P("var", "ind"), P(), P("ind", None, None), P("ind"), P("ind"), P("ind"))
    return jax.shard_map(
        local,
        mesh=mesh,
        in_specs=placed,
        out_specs=(P("var", "ind"), P("var", None)),
        check_vma=False,
    )
```

```python
import jax
import jax.numpy as jnp
from jax import lax
from jax.sharding import PartitionSpec as P

VARS_GENE = 4
NEED = 2
PAD_ROWS = 8
CHUNKS = 1


def split2(x):
    hi = lax.reduce_precision(x, exponent_bits=8, mantissa_bits=7)
    lo = x - hi
    return hi.astype(jnp.bfloat16), lo.astype(jnp.bfloat16)


def batched_tile_dot(lhs, tiles):
    cols = lhs.shape[1]
    parts = jnp.concatenate(split2(lhs), axis=1)
    prod = lax.dot_general(
        parts, tiles, (((2,), (2,)), ((0,), (0,))), preferred_element_type=jnp.float32
    )
    return prod[:, :cols] + prod[:, cols:]


def local(genotypes, variance_comp, grm_tiles, tile_rows, tile_cols, tile_live):
    cols_here, rows_here = genotypes.shape
    tile_size = grm_tiles.shape[1]
    slot_count = grm_tiles.shape[0]
    row_tiles = rows_here // tile_size
    off_count = slot_count - row_tiles
    me = lax.axis_index("ind")
    peers = lax.axis_size("ind")
    v = lax.axis_index("var")
    nvar = lax.axis_size("var")
    ncol = cols_here * nvar
    genes = ncol // VARS_GENE
    total_ind = peers * rows_here
    tau0 = variance_comp[0]
    tau1 = variance_comp[1]
    live = tile_live[0]

    eye = jnp.arange(tile_size)[:, None] == jnp.arange(tile_size)[None, :]
    diag_values = jnp.sum(
        jnp.where(eye[None], grm_tiles[:row_tiles].astype(jnp.float32), 0.0), axis=2
    )
    precond = (tau0 + tau1 * diag_values)[:, None, :]
    off_rows = tile_rows[row_tiles:]
    off_cols = tile_cols[row_tiles:]
    live_mask = (jnp.arange(row_tiles, slot_count, dtype=jnp.int32) < live).astype(jnp.float32)
    weight = (off_rows[:, None] == jnp.arange(row_tiles, dtype=jnp.int32)[None, :]).astype(jnp.float32)
    weight = weight * live_mask[:, None]
    position = off_cols // row_tiles * NEED + (off_cols % row_tiles - me) % row_tiles
    position = jnp.clip(position, 0, peers * NEED - 1)

    def to_tiles(x):
        return jnp.transpose(x.reshape(cols_here, row_tiles, tile_size), (1, 0, 2))

    def from_tiles(x):
        return jnp.transpose(x, (1, 0, 2)).reshape(cols_here, rows_here)

    def exchange(x, extra):
        rolled = jnp.stack([jnp.roll(x, -t, axis=0) for t in range(NEED)], axis=1)
        width = x.shape[1]
        rolled = rolled.reshape(row_tiles, NEED * width, tile_size)
        pieces = jnp.tile(rolled, (peers // row_tiles, 1, 1))
        if extra is not None:
            flat = extra.reshape(-1)
            flat = jnp.pad(flat, (0, PAD_ROWS * tile_size - flat.shape[0]))
            side = jnp.broadcast_to(flat.reshape(1, PAD_ROWS, tile_size), (peers, PAD_ROWS, tile_size))
            pieces = jnp.concatenate([pieces, side], axis=1)
        arrived = lax.all_to_all(pieces, "ind", split_axis=0, concat_axis=0, tiled=True)
        if extra is None:
            return arrived.reshape(peers * NEED, width, tile_size), None
        tiles_in = arrived[:, :NEED * width].reshape(peers * NEED, width, tile_size)
        sums = jnp.sum(arrived[:, NEED * width:].reshape(peers, -1)[:, :extra.size], axis=0)
        return tiles_in, sums.reshape(extra.shape)

    def kprod(x, arrived):
        width = x.shape[1]
        picked = jnp.stack([lax.dynamic_index_in_dim(arrived, position[s], 0, keepdims=False)
                            for s in range(off_count)])
        near = batched_tile_dot(x, grm_tiles[:row_tiles])
        far = batched_tile_dot(picked, grm_tiles[row_tiles:])
        return near + jnp.sum(weight[:, :, None, None] * far[:, None], axis=0)

    def colsum(x):
        return jnp.sum(x, axis=(0, 2))

    geno_all = lax.all_gather(genotypes, "var", axis=0, tiled=True)
    first = v * cols_here
    a_out = first // genes
    g0 = first % genes
    geno_sub = jnp.stack(
        [to_tiles(lax.dynamic_slice_in_dim(geno_all, a * genes + g0, cols_here, 0))
         for a in range(VARS_GENE)]
    )

    def chunk(g, geno_sub):
        z0 = g / precond
        tiles0, sums0 = exchange(z0, colsum(g * z0)[None])
        rz0 = sums0[0]
        kz0 = kprod(z0, tiles0)
        image0 = tau0 * z0 + tau1 * kz0
        w = image0 / precond
        p0_local = jnp.sum(geno_sub * z0[None], axis=(1, 3))
        extra1 = jnp.concatenate([colsum(z0 * image0)[None], p0_local], axis=0)
        tiles1, sums1 = exchange(w, extra1)
        dad0 = sums1[0]
        p0 = sums1[1:]
        alpha0 = rz0 / dad0
        resid1 = g - alpha0[None, :, None] * image0
        z1 = resid1 / precond
        kw = kprod(w, tiles1)
        kz1 = kz0 - alpha0[None, :, None] * kw
        az1 = tau0 * z1 + tau1 * kz1
        red_local = jnp.concatenate(
            [colsum(resid1 * z1)[None], colsum(z1 * az1)[None],
             colsum(z1 * image0 + z0 * az1)[None], jnp.sum(geno_sub * z1[None], axis=(1, 3))],
            axis=0,
        )
        lead = (me == 0).astype(jnp.float32)
        payload = jnp.concatenate(
            [red_local, lead * rz0[None], lead * dad0[None], lead * p0], axis=0)
        spread = jnp.broadcast_to(payload[None], (peers * nvar,) + payload.shape)
        got = lax.all_to_all(spread, ("ind", "var"), split_axis=0, concat_axis=0, tiled=True)
        tot = jnp.sum(got.reshape((peers, nvar) + payload.shape), axis=0)
        nv = VARS_GENE
        rz1_all = tot[:, 0]
        rz0_all = tot[:, 3 + nv]
        dad0_all = tot[:, 4 + nv]
        p0_all = tot[:, 5 + nv:]
        p1_all = tot[:, 3:3 + nv]
        alpha0_all = rz0_all / dad0_all
        beta_all = rz1_all / rz0_all
        dad1_all = tot[:, 1] + beta_all * (tot[:, 2] + beta_all * dad0_all)
        alpha1_all = rz1_all / dad1_all
        mine = lambda t: lax.dynamic_index_in_dim(t, v, 0, keepdims=False)
        beta = mine(beta_all)
        alpha1 = mine(alpha1_all)
        dir1 = z1 + beta[None, :, None] * z0
        sol = alpha0[None, :, None] * z0 + alpha1[None, :, None] * dir1
        part = alpha0_all[:, None] * p0_all + alpha1_all[:, None] * (p1_all + beta_all[:, None] * p0_all)
        return sol, part

    g_all = to_tiles(genotypes)
    width = cols_here // CHUNKS
    outs = [chunk(g_all[:, k * width:(k + 1) * width], geno_sub[:, :, k * width:(k + 1) * width])
            for k in range(CHUNKS)]
    solution = jnp.concatenate([o[0] for o in outs], axis=1)
    gram_part = jnp.concatenate([o[1] for o in outs], axis=2)
    full = jnp.transpose(gram_part, (1, 0, 2)).reshape(VARS_GENE, ncol)
    gram_cols = lax.dynamic_index_in_dim(full, a_out, 0, keepdims=False)
    gram_cols = lax.dynamic_slice_in_dim(gram_cols.reshape(VARS_GENE, genes), g0, cols_here, 1)
    gene_gram = jnp.transpose(gram_cols) / total_ind
    return (from_tiles(solution), gene_gram)


def solution(mesh):
    placed = (P("var", "ind"), P(), P("ind", None, None), P("ind"), P("ind"), P("ind"))
    return jax.shard_map(
        local,
        mesh=mesh,
        in_specs=placed,
        out_specs=(P("var", "ind"), P("var", None)),
        check_vma=False,
    )
```

```python
import jax
import jax.numpy as jnp
from jax import lax
from jax.sharding import PartitionSpec as P

VARS_GENE = 4
NEED = 2
PAD_ROWS = 8
CHUNKS = 1


def split2(x):
    hi = lax.reduce_precision(x, exponent_bits=8, mantissa_bits=7)
    lo = x - hi
    return hi.astype(jnp.bfloat16), lo.astype(jnp.bfloat16)


def batched_tile_dot(lhs, tiles):
    cols = lhs.shape[1]
    parts = jnp.concatenate(split2(lhs), axis=1)
    prod = lax.dot_general(
        parts, tiles, (((2,), (2,)), ((0,), (0,))), preferred_element_type=jnp.float32
    )
    return prod[:, :cols] + prod[:, cols:]


def local(genotypes, variance_comp, grm_tiles, tile_rows, tile_cols, tile_live):
    cols_here, rows_here = genotypes.shape
    tile_size = grm_tiles.shape[1]
    slot_count = grm_tiles.shape[0]
    row_tiles = rows_here // tile_size
    off_count = slot_count - row_tiles
    me = lax.axis_index("ind")
    peers = lax.axis_size("ind")
    v = lax.axis_index("var")
    nvar = lax.axis_size("var")
    ncol = cols_here * nvar
    genes = ncol // VARS_GENE
    total_ind = peers * rows_here
    tau0 = variance_comp[0]
    tau1 = variance_comp[1]
    live = tile_live[0]

    eye = jnp.arange(tile_size)[:, None] == jnp.arange(tile_size)[None, :]
    diag_values = jnp.sum(
        jnp.where(eye[None], grm_tiles[:row_tiles].astype(jnp.float32), 0.0), axis=2
    )
    precond = (tau0 + tau1 * diag_values)[:, None, :]
    off_rows = tile_rows[row_tiles:]
    off_cols = tile_cols[row_tiles:]
    live_mask = (jnp.arange(row_tiles, slot_count, dtype=jnp.int32) < live).astype(jnp.float32)
    weight = (off_rows[:, None] == jnp.arange(row_tiles, dtype=jnp.int32)[None, :]).astype(jnp.float32)
    weight = weight * live_mask[:, None]
    position = off_cols // row_tiles * NEED + (off_cols % row_tiles - me) % row_tiles
    position = jnp.clip(position, 0, peers * NEED - 1)

    def to_tiles(x):
        return jnp.transpose(x.reshape(cols_here, row_tiles, tile_size), (1, 0, 2))

    def from_tiles(x):
        return jnp.transpose(x, (1, 0, 2)).reshape(cols_here, rows_here)

    def exchange(x, extra):
        width = x.shape[1]
        side = []
        if extra is not None:
            flat = extra.reshape(-1)
            flat = jnp.pad(flat, (0, PAD_ROWS * tile_size - flat.shape[0]))
            side = [flat.reshape(PAD_ROWS, tile_size)]
        rows = []
        for p in range(peers):
            rows += [x[(p + t) % row_tiles] for t in range(NEED)] + side
        pieces = jnp.concatenate(rows, axis=0).reshape(peers, -1, tile_size)
        arrived = lax.all_to_all(pieces, "ind", split_axis=0, concat_axis=0, tiled=True)
        if extra is None:
            return arrived.reshape(peers * NEED, width, tile_size), None
        tiles_in = arrived[:, :NEED * width].reshape(peers * NEED, width, tile_size)
        sums = jnp.sum(arrived[:, NEED * width:].reshape(peers, -1)[:, :extra.size], axis=0)
        return tiles_in, sums.reshape(extra.shape)

    def kprod(x, arrived):
        width = x.shape[1]
        picked = jnp.take(arrived, position, axis=0, mode="clip")
        near = batched_tile_dot(x, grm_tiles[:row_tiles])
        far = batched_tile_dot(picked, grm_tiles[row_tiles:])
        return near + jnp.sum(weight[:, :, None, None] * far[:, None], axis=0)

    def colsum(x):
        return jnp.sum(x, axis=(0, 2))

    geno_all = lax.all_gather(genotypes, "var", axis=0, tiled=True)
    first = v * cols_here
    a_out = first // genes
    g0 = first % genes
    geno_sub = jnp.stack(
        [to_tiles(lax.dynamic_slice_in_dim(geno_all, a * genes + g0, cols_here, 0))
         for a in range(VARS_GENE)]
    )

    def chunk(g, geno_sub):
        z0 = g / precond
        tiles0, _ = exchange(z0, None)
        kz0 = kprod(z0, tiles0)
        image0 = tau0 * z0 + tau1 * kz0
        w = image0 / precond
        p0_local = jnp.sum(geno_sub * z0[None], axis=(1, 3))
        extra1 = jnp.concatenate([colsum(g * z0)[None], colsum(z0 * image0)[None], p0_local], axis=0)
        tiles1, sums1 = exchange(w, extra1)
        rz0 = sums1[0]
        dad0 = sums1[1]
        p0 = sums1[2:]
        alpha0 = rz0 / dad0
        resid1 = g - alpha0[None, :, None] * image0
        z1 = resid1 / precond
        kw = kprod(w, tiles1)
        kz1 = kz0 - alpha0[None, :, None] * kw
        az1 = tau0 * z1 + tau1 * kz1
        red_local = jnp.concatenate(
            [colsum(resid1 * z1)[None], colsum(z1 * az1)[None],
             colsum(z1 * image0 + z0 * az1)[None], jnp.sum(geno_sub * z1[None], axis=(1, 3))],
            axis=0,
        )
        lead = (me == 0).astype(jnp.float32)
        payload = jnp.concatenate(
            [red_local, lead * rz0[None], lead * dad0[None], lead * p0], axis=0)
        spread = jnp.broadcast_to(payload[None], (peers * nvar,) + payload.shape)
        got = lax.all_to_all(spread, ("ind", "var"), split_axis=0, concat_axis=0, tiled=True)
        tot = jnp.sum(got.reshape((peers, nvar) + payload.shape), axis=0)
        nv = VARS_GENE
        rz1_all = tot[:, 0]
        rz0_all = tot[:, 3 + nv]
        dad0_all = tot[:, 4 + nv]
        p0_all = tot[:, 5 + nv:]
        p1_all = tot[:, 3:3 + nv]
        alpha0_all = rz0_all / dad0_all
        beta_all = rz1_all / rz0_all
        dad1_all = tot[:, 1] + beta_all * (tot[:, 2] + beta_all * dad0_all)
        alpha1_all = rz1_all / dad1_all
        mine = lambda t: lax.dynamic_index_in_dim(t, v, 0, keepdims=False)
        beta = mine(beta_all)
        alpha1 = mine(alpha1_all)
        dir1 = z1 + beta[None, :, None] * z0
        sol = alpha0[None, :, None] * z0 + alpha1[None, :, None] * dir1
        part = alpha0_all[:, None] * p0_all + alpha1_all[:, None] * (p1_all + beta_all[:, None] * p0_all)
        return sol, part

    g_all = to_tiles(genotypes)
    width = cols_here // CHUNKS
    outs = [chunk(g_all[:, k * width:(k + 1) * width], geno_sub[:, :, k * width:(k + 1) * width])
            for k in range(CHUNKS)]
    solution = jnp.concatenate([o[0] for o in outs], axis=1)
    gram_part = jnp.concatenate([o[1] for o in outs], axis=2)
    full = jnp.transpose(gram_part, (1, 0, 2)).reshape(VARS_GENE, ncol)
    gram_cols = lax.dynamic_index_in_dim(full, a_out, 0, keepdims=False)
    gram_cols = lax.dynamic_slice_in_dim(gram_cols.reshape(VARS_GENE, genes), g0, cols_here, 1)
    gene_gram = jnp.transpose(gram_cols) / total_ind
    return (from_tiles(solution), gene_gram)


def solution(mesh):
    placed = (P("var", "ind"), P(), P("ind", None, None), P("ind"), P("ind"), P("ind"))
    return jax.shard_map(
        local,
        mesh=mesh,
        in_specs=placed,
        out_specs=(P("var", "ind"), P("var", None)),
        check_vma=False,
    )
```

```python
import jax
import jax.numpy as jnp
from jax import lax
from jax.sharding import PartitionSpec as P

VARS_GENE = 4
NEED = 2
PAD_ROWS = 8
CHUNKS = 1


def split2(x):
    hi = lax.reduce_precision(x, exponent_bits=8, mantissa_bits=7)
    lo = x - hi
    return hi.astype(jnp.bfloat16), lo.astype(jnp.bfloat16)


def batched_tile_dot(lhs, tiles):
    cols = lhs.shape[1]
    parts = jnp.concatenate(split2(lhs), axis=1)
    prod = lax.dot_general(
        parts, tiles, (((2,), (2,)), ((0,), (0,))), preferred_element_type=jnp.float32
    )
    return prod[:, :cols] + prod[:, cols:]


def local(genotypes, variance_comp, grm_tiles, tile_rows, tile_cols, tile_live):
    cols_here, rows_here = genotypes.shape
    tile_size = grm_tiles.shape[1]
    slot_count = grm_tiles.shape[0]
    row_tiles = rows_here // tile_size
    off_count = slot_count - row_tiles
    me = lax.axis_index("ind")
    peers = lax.axis_size("ind")
    v = lax.axis_index("var")
    nvar = lax.axis_size("var")
    ncol = cols_here * nvar
    genes = ncol // VARS_GENE
    total_ind = peers * rows_here
    tau0 = variance_comp[0]
    tau1 = variance_comp[1]
    live = tile_live[0]

    eye = jnp.arange(tile_size)[:, None] == jnp.arange(tile_size)[None, :]
    diag_values = jnp.sum(
        jnp.where(eye[None], grm_tiles[:row_tiles].astype(jnp.float32), 0.0), axis=2
    )
    precond = (tau0 + tau1 * diag_values)[:, None, :]
    off_rows = tile_rows[row_tiles:]
    off_cols = tile_cols[row_tiles:]
    live_mask = (jnp.arange(row_tiles, slot_count, dtype=jnp.int32) < live).astype(jnp.float32)
    weight = (off_rows[:, None] == jnp.arange(row_tiles, dtype=jnp.int32)[None, :]).astype(jnp.float32)
    weight = weight * live_mask[:, None]
    position = off_cols // row_tiles * NEED + (off_cols % row_tiles - me) % row_tiles
    position = jnp.clip(position, 0, peers * NEED - 1)

    def to_tiles(x):
        return jnp.transpose(x.reshape(cols_here, row_tiles, tile_size), (1, 0, 2))

    def from_tiles(x):
        return jnp.transpose(x, (1, 0, 2)).reshape(cols_here, rows_here)

    def exchange(x, extra, by_concat=False):
        width = x.shape[1]
        flat = extra.reshape(-1)
        flat = jnp.pad(flat, (0, PAD_ROWS * tile_size - flat.shape[0]))
        if by_concat:
            rows = []
            for p in range(peers):
                rows += [x[(p + t) % row_tiles] for t in range(NEED)]
                rows.append(flat.reshape(PAD_ROWS, tile_size))
            pieces = jnp.concatenate(rows, axis=0).reshape(peers, -1, tile_size)
        else:
            rolled = jnp.stack([jnp.roll(x, -t, axis=0) for t in range(NEED)], axis=1)
            rolled = rolled.reshape(row_tiles, NEED * width, tile_size)
            pieces = jnp.tile(rolled, (peers // row_tiles, 1, 1))
            side = jnp.broadcast_to(flat.reshape(1, PAD_ROWS, tile_size), (peers, PAD_ROWS, tile_size))
            pieces = jnp.concatenate([pieces, side], axis=1)
        arrived = lax.all_to_all(pieces, "ind", split_axis=0, concat_axis=0, tiled=True)
        tiles_in = arrived[:, :NEED * width].reshape(peers * NEED, width, tile_size)
        sums = jnp.sum(arrived[:, NEED * width:].reshape(peers, -1)[:, :extra.size], axis=0)
        return tiles_in, sums.reshape(extra.shape)

    def kprod(x, arrived):
        width = x.shape[1]
        picked = jnp.stack([lax.dynamic_index_in_dim(arrived, position[s], 0, keepdims=False)
                            for s in range(off_count)])
        near = batched_tile_dot(x, grm_tiles[:row_tiles])
        far = batched_tile_dot(picked, grm_tiles[row_tiles:])
        return near + jnp.sum(weight[:, :, None, None] * far[:, None], axis=0)

    def colsum(x):
        return jnp.sum(x, axis=(0, 2))

    geno_all = lax.all_gather(genotypes, "var", axis=0, tiled=True)
    first = v * cols_here
    a_out = first // genes
    g0 = first % genes
    geno_sub = jnp.stack(
        [to_tiles(lax.dynamic_slice_in_dim(geno_all, a * genes + g0, cols_here, 0))
         for a in range(VARS_GENE)]
    )

    def chunk(g, geno_sub):
        z0 = g / precond
        tiles0, sums0 = exchange(z0, colsum(g * z0)[None])
        rz0 = sums0[0]
        kz0 = kprod(z0, tiles0)
        image0 = tau0 * z0 + tau1 * kz0
        w = image0 / precond
        p0_local = jnp.sum(geno_sub * z0[None], axis=(1, 3))
        extra1 = jnp.concatenate([colsum(z0 * image0)[None], p0_local], axis=0)
        tiles1, sums1 = exchange(w, extra1, by_concat=True)
        dad0 = sums1[0]
        p0 = sums1[1:]
        alpha0 = rz0 / dad0
        resid1 = g - alpha0[None, :, None] * image0
        z1 = resid1 / precond
        kw = kprod(w, tiles1)
        kz1 = kz0 - alpha0[None, :, None] * kw
        az1 = tau0 * z1 + tau1 * kz1
        red_local = jnp.concatenate(
            [colsum(resid1 * z1)[None], colsum(z1 * az1)[None],
             colsum(z1 * image0 + z0 * az1)[None], jnp.sum(geno_sub * z1[None], axis=(1, 3))],
            axis=0,
        )
        lead = (me == 0).astype(jnp.float32)
        payload = jnp.concatenate(
            [red_local, lead * rz0[None], lead * dad0[None], lead * p0], axis=0)
        spread = jnp.broadcast_to(payload[None], (peers * nvar,) + payload.shape)
        got = lax.all_to_all(spread, ("ind", "var"), split_axis=0, concat_axis=0, tiled=True)
        tot = jnp.sum(got.reshape((peers, nvar) + payload.shape), axis=0)
        nv = VARS_GENE
        rz1_all = tot[:, 0]
        rz0_all = tot[:, 3 + nv]
        dad0_all = tot[:, 4 + nv]
        p0_all = tot[:, 5 + nv:]
        p1_all = tot[:, 3:3 + nv]
        alpha0_all = rz0_all / dad0_all
        beta_all = rz1_all / rz0_all
        dad1_all = tot[:, 1] + beta_all * (tot[:, 2] + beta_all * dad0_all)
        alpha1_all = rz1_all / dad1_all
        mine = lambda t: lax.dynamic_index_in_dim(t, v, 0, keepdims=False)
        beta = mine(beta_all)
        alpha1 = mine(alpha1_all)
        dir1 = z1 + beta[None, :, None] * z0
        sol = alpha0[None, :, None] * z0 + alpha1[None, :, None] * dir1
        part = alpha0_all[:, None] * p0_all + alpha1_all[:, None] * (p1_all + beta_all[:, None] * p0_all)
        return sol, part

    g_all = to_tiles(genotypes)
    width = cols_here // CHUNKS
    outs = [chunk(g_all[:, k * width:(k + 1) * width], geno_sub[:, :, k * width:(k + 1) * width])
            for k in range(CHUNKS)]
    solution = jnp.concatenate([o[0] for o in outs], axis=1)
    gram_part = jnp.concatenate([o[1] for o in outs], axis=2)
    full = jnp.transpose(gram_part, (1, 0, 2)).reshape(VARS_GENE, ncol)
    gram_cols = lax.dynamic_index_in_dim(full, a_out, 0, keepdims=False)
    gram_cols = lax.dynamic_slice_in_dim(gram_cols.reshape(VARS_GENE, genes), g0, cols_here, 1)
    gene_gram = jnp.transpose(gram_cols) / total_ind
    return (from_tiles(solution), gene_gram)


def solution(mesh):
    placed = (P("var", "ind"), P(), P("ind", None, None), P("ind"), P("ind"), P("ind"))
    return jax.shard_map(
        local,
        mesh=mesh,
        in_specs=placed,
        out_specs=(P("var", "ind"), P("var", None)),
        check_vma=False,
    )
```

```python
import jax
import jax.numpy as jnp
from jax import lax
from jax.sharding import PartitionSpec as P
from jax.experimental import pallas as pl
from jax.experimental.pallas import tpu as pltpu

VARS_GENE = 4
NEED = 2
PAD_ROWS = 8
CHUNKS = 1


def split2(x):
    hi = lax.reduce_precision(x, exponent_bits=8, mantissa_bits=7)
    lo = x - hi
    return hi.astype(jnp.bfloat16), lo.astype(jnp.bfloat16)


def batched_tile_dot(lhs, tiles):
    cols = lhs.shape[1]
    parts = jnp.concatenate(split2(lhs), axis=1)
    prod = lax.dot_general(
        parts, tiles, (((2,), (2,)), ((0,), (0,))), preferred_element_type=jnp.float32
    )
    return prod[:, :cols] + prod[:, cols:]


def far_kernel(pos_ref, rows_ref, nlive_ref, a_ref, t_ref, o_ref):
    s = pl.program_id(0)

    @pl.when(s == 0)
    def _():
        o_ref[...] = jnp.zeros_like(o_ref)

    @pl.when(s < nlive_ref[0])
    def _():
        x = a_ref[0]
        hi = x.astype(jnp.bfloat16)
        lo = (x - hi.astype(jnp.float32)).astype(jnp.bfloat16)
        tile = t_ref[0]
        dims = (((1,), (1,)), ((), ()))
        prod = lax.dot_general(hi, tile, dims, preferred_element_type=jnp.float32)
        prod = prod + lax.dot_general(lo, tile, dims, preferred_element_type=jnp.float32)
        r = rows_ref[s]
        o_ref[r] = o_ref[r] + prod


def far_product(arrived, tiles, pos, rows, nlive, width, row_tiles):
    off_count = pos.shape[0]
    tile_size = tiles.shape[1]
    grid_spec = pltpu.PrefetchScalarGridSpec(
        num_scalar_prefetch=3,
        grid=(off_count,),
        in_specs=[
            pl.BlockSpec((1, width, tile_size),
                         lambda s, p, r, n: (p[s] // NEED, p[s] % NEED, 0)),
            pl.BlockSpec((1, tile_size, tile_size), lambda s, p, r, n: (row_tiles + s, 0, 0)),
        ],
        out_specs=pl.BlockSpec((row_tiles, width, tile_size), lambda s, p, r, n: (0, 0, 0)),
    )
    cost = pl.CostEstimate(
        flops=off_count * 4 * width * tile_size * tile_size,
        transcendentals=0,
        bytes_accessed=off_count * (tile_size * tile_size * 2 + width * tile_size * 4)
        + row_tiles * width * tile_size * 4,
    )
    return pl.pallas_call(
        far_kernel,
        grid_spec=grid_spec,
        out_shape=jax.ShapeDtypeStruct((row_tiles, width, tile_size), jnp.float32),
        compiler_params=pltpu.CompilerParams(dimension_semantics=("arbitrary",)),
        cost_estimate=cost,
    )(pos, rows, nlive, arrived, tiles)


def local(genotypes, variance_comp, grm_tiles, tile_rows, tile_cols, tile_live):
    cols_here, rows_here = genotypes.shape
    tile_size = grm_tiles.shape[1]
    slot_count = grm_tiles.shape[0]
    row_tiles = rows_here // tile_size
    off_count = slot_count - row_tiles
    me = lax.axis_index("ind")
    peers = lax.axis_size("ind")
    v = lax.axis_index("var")
    nvar = lax.axis_size("var")
    ncol = cols_here * nvar
    genes = ncol // VARS_GENE
    total_ind = peers * rows_here
    tau0 = variance_comp[0]
    tau1 = variance_comp[1]
    live = tile_live[0]

    eye = jnp.arange(tile_size)[:, None] == jnp.arange(tile_size)[None, :]
    diag_values = jnp.sum(
        jnp.where(eye[None], grm_tiles[:row_tiles].astype(jnp.float32), 0.0), axis=2
    )
    precond = (tau0 + tau1 * diag_values)[:, None, :]
    off_rows = tile_rows[row_tiles:]
    off_cols = tile_cols[row_tiles:]
    live_mask = (jnp.arange(row_tiles, slot_count, dtype=jnp.int32) < live).astype(jnp.float32)
    weight = (off_rows[:, None] == jnp.arange(row_tiles, dtype=jnp.int32)[None, :]).astype(jnp.float32)
    weight = weight * live_mask[:, None]
    position = off_cols // row_tiles * NEED + (off_cols % row_tiles - me) % row_tiles
    position = jnp.clip(position, 0, peers * NEED - 1)
    rows_safe = jnp.clip(off_rows, 0, row_tiles - 1)
    nlive = jnp.reshape(live - row_tiles, (1,))

    def to_tiles(x):
        return jnp.transpose(x.reshape(cols_here, row_tiles, tile_size), (1, 0, 2))

    def from_tiles(x):
        return jnp.transpose(x, (1, 0, 2)).reshape(cols_here, rows_here)

    def exchange(x, extra, by_concat=False):
        width = x.shape[1]
        flat = extra.reshape(-1)
        flat = jnp.pad(flat, (0, PAD_ROWS * tile_size - flat.shape[0]))
        if by_concat:
            rows = []
            for p in range(peers):
                rows += [x[(p + t) % row_tiles] for t in range(NEED)]
                rows.append(flat.reshape(PAD_ROWS, tile_size))
            pieces = jnp.concatenate(rows, axis=0).reshape(peers, -1, tile_size)
        else:
            rolled = jnp.stack([jnp.roll(x, -t, axis=0) for t in range(NEED)], axis=1)
            rolled = rolled.reshape(row_tiles, NEED * width, tile_size)
            pieces = jnp.tile(rolled, (peers // row_tiles, 1, 1))
            side = jnp.broadcast_to(flat.reshape(1, PAD_ROWS, tile_size), (peers, PAD_ROWS, tile_size))
            pieces = jnp.concatenate([pieces, side], axis=1)
        arrived = lax.all_to_all(pieces, "ind", split_axis=0, concat_axis=0, tiled=True)
        sums = jnp.sum(arrived[:, NEED * width:].reshape(peers, -1)[:, :extra.size], axis=0)
        return arrived, sums.reshape(extra.shape)

    def kprod(x, arrived):
        near = batched_tile_dot(x, grm_tiles[:row_tiles])
        far = far_product(arrived, grm_tiles, position, rows_safe, nlive, x.shape[1], row_tiles)
        return near + far

    def colsum(x):
        return jnp.sum(x, axis=(0, 2))

    geno_all = lax.all_gather(genotypes, "var", axis=0, tiled=True)
    first = v * cols_here
    a_out = first // genes
    g0 = first % genes
    geno_sub = jnp.stack(
        [to_tiles(lax.dynamic_slice_in_dim(geno_all, a * genes + g0, cols_here, 0))
         for a in range(VARS_GENE)]
    )

    def chunk(g, geno_sub):
        z0 = g / precond
        tiles0, sums0 = exchange(z0, colsum(g * z0)[None])
        rz0 = sums0[0]
        kz0 = kprod(z0, tiles0)
        image0 = tau0 * z0 + tau1 * kz0
        w = image0 / precond
        p0_local = jnp.sum(geno_sub * z0[None], axis=(1, 3))
        extra1 = jnp.concatenate([colsum(z0 * image0)[None], p0_local], axis=0)
        tiles1, sums1 = exchange(w, extra1, by_concat=True)
        dad0 = sums1[0]
        p0 = sums1[1:]
        alpha0 = rz0 / dad0
        resid1 = g - alpha0[None, :, None] * image0
        z1 = resid1 / precond
        kw = kprod(w, tiles1)
        kz1 = kz0 - alpha0[None, :, None] * kw
        az1 = tau0 * z1 + tau1 * kz1
        red_local = jnp.concatenate(
            [colsum(resid1 * z1)[None], colsum(z1 * az1)[None],
             colsum(z1 * image0 + z0 * az1)[None], jnp.sum(geno_sub * z1[None], axis=(1, 3))],
            axis=0,
        )
        lead = (me == 0).astype(jnp.float32)
        payload = jnp.concatenate(
            [red_local, lead * rz0[None], lead * dad0[None], lead * p0], axis=0)
        spread = jnp.broadcast_to(payload[None], (peers * nvar,) + payload.shape)
        got = lax.all_to_all(spread, ("ind", "var"), split_axis=0, concat_axis=0, tiled=True)
        tot = jnp.sum(got.reshape((peers, nvar) + payload.shape), axis=0)
        nv = VARS_GENE
        rz1_all = tot[:, 0]
        rz0_all = tot[:, 3 + nv]
        dad0_all = tot[:, 4 + nv]
        p0_all = tot[:, 5 + nv:]
        p1_all = tot[:, 3:3 + nv]
        alpha0_all = rz0_all / dad0_all
        beta_all = rz1_all / rz0_all
        dad1_all = tot[:, 1] + beta_all * (tot[:, 2] + beta_all * dad0_all)
        alpha1_all = rz1_all / dad1_all
        mine = lambda t: lax.dynamic_index_in_dim(t, v, 0, keepdims=False)
        beta = mine(beta_all)
        alpha1 = mine(alpha1_all)
        dir1 = z1 + beta[None, :, None] * z0
        sol = alpha0[None, :, None] * z0 + alpha1[None, :, None] * dir1
        part = alpha0_all[:, None] * p0_all + alpha1_all[:, None] * (p1_all + beta_all[:, None] * p0_all)
        return sol, part

    g_all = to_tiles(genotypes)
    width = cols_here // CHUNKS
    outs = [chunk(g_all[:, k * width:(k + 1) * width], geno_sub[:, :, k * width:(k + 1) * width])
            for k in range(CHUNKS)]
    solution = jnp.concatenate([o[0] for o in outs], axis=1)
    gram_part = jnp.concatenate([o[1] for o in outs], axis=2)
    full = jnp.transpose(gram_part, (1, 0, 2)).reshape(VARS_GENE, ncol)
    gram_cols = lax.dynamic_index_in_dim(full, a_out, 0, keepdims=False)
    gram_cols = lax.dynamic_slice_in_dim(gram_cols.reshape(VARS_GENE, genes), g0, cols_here, 1)
    gene_gram = jnp.transpose(gram_cols) / total_ind
    return (from_tiles(solution), gene_gram)


def solution(mesh):
    placed = (P("var", "ind"), P(), P("ind", None, None), P("ind"), P("ind"), P("ind"))
    return jax.shard_map(
        local,
        mesh=mesh,
        in_specs=placed,
        out_specs=(P("var", "ind"), P("var", None)),
        check_vma=False,
    )
```

```python
import jax
import jax.numpy as jnp
from jax import lax
from jax.sharding import PartitionSpec as P

VARS_GENE = 4
NEED = 2
PAD_ROWS = 8
CHUNKS = 1


def split2(x):
    hi = lax.reduce_precision(x, exponent_bits=8, mantissa_bits=7)
    lo = x - hi
    return hi.astype(jnp.bfloat16), lo.astype(jnp.bfloat16)


def batched_tile_dot(lhs, tiles):
    cols = lhs.shape[1]
    parts = jnp.concatenate(split2(lhs), axis=1)
    prod = lax.dot_general(
        parts, tiles, (((2,), (2,)), ((0,), (0,))), preferred_element_type=jnp.float32
    )
    return prod[:, :cols] + prod[:, cols:]


def local(genotypes, variance_comp, grm_tiles, tile_rows, tile_cols, tile_live):
    cols_here, rows_here = genotypes.shape
    tile_size = grm_tiles.shape[1]
    slot_count = grm_tiles.shape[0]
    row_tiles = rows_here // tile_size
    off_count = slot_count - row_tiles
    me = lax.axis_index("ind")
    peers = lax.axis_size("ind")
    v = lax.axis_index("var")
    nvar = lax.axis_size("var")
    ncol = cols_here * nvar
    genes = ncol // VARS_GENE
    total_ind = peers * rows_here
    tau0 = variance_comp[0]
    tau1 = variance_comp[1]
    live = tile_live[0]

    lane = 128
    nblk = tile_size // lane
    split_tiles = grm_tiles[:row_tiles].reshape(row_tiles, nblk, lane, nblk, lane)
    diag_blocks = jnp.stack([split_tiles[:, b, :, b, :] for b in range(nblk)], axis=1)
    eye = jnp.arange(lane)[:, None] == jnp.arange(lane)[None, :]
    diag_values = jnp.sum(
        jnp.where(eye[None, None], diag_blocks.astype(jnp.float32), 0.0), axis=2
    ).reshape(row_tiles, tile_size)
    precond = (tau0 + tau1 * diag_values)[:, None, :]
    off_rows = tile_rows[row_tiles:]
    off_cols = tile_cols[row_tiles:]
    live_mask = (jnp.arange(row_tiles, slot_count, dtype=jnp.int32) < live).astype(jnp.float32)
    weight = (off_rows[:, None] == jnp.arange(row_tiles, dtype=jnp.int32)[None, :]).astype(jnp.float32)
    weight = weight * live_mask[:, None]
    position = off_cols // row_tiles * NEED + (off_cols % row_tiles - me) % row_tiles
    position = jnp.clip(position, 0, peers * NEED - 1)

    def to_tiles(x):
        return jnp.transpose(x.reshape(cols_here, row_tiles, tile_size), (1, 0, 2))

    def from_tiles(x):
        return jnp.transpose(x, (1, 0, 2)).reshape(cols_here, rows_here)

    def exchange(x, extra, by_concat=False):
        width = x.shape[1]
        flat = extra.reshape(-1)
        flat = jnp.pad(flat, (0, PAD_ROWS * tile_size - flat.shape[0]))
        if by_concat:
            rows = []
            for p in range(peers):
                rows += [x[(p + t) % row_tiles] for t in range(NEED)]
                rows.append(flat.reshape(PAD_ROWS, tile_size))
            pieces = jnp.concatenate(rows, axis=0).reshape(peers, -1, tile_size)
        else:
            rolled = jnp.stack([jnp.roll(x, -t, axis=0) for t in range(NEED)], axis=1)
            rolled = rolled.reshape(row_tiles, NEED * width, tile_size)
            pieces = jnp.tile(rolled, (peers // row_tiles, 1, 1))
            side = jnp.broadcast_to(flat.reshape(1, PAD_ROWS, tile_size), (peers, PAD_ROWS, tile_size))
            pieces = jnp.concatenate([pieces, side], axis=1)
        arrived = lax.all_to_all(pieces, "ind", split_axis=0, concat_axis=0, tiled=True)
        sums = jnp.sum(arrived[:, NEED * width:].reshape(peers, -1)[:, :extra.size], axis=0)
        return arrived, sums.reshape(extra.shape)

    def kprod(x, arrived):
        width = x.shape[1]
        sub = 8
        view = arrived.reshape(peers, arrived.shape[1] // sub, sub, tile_size)
        picked = jnp.stack([
            lax.dynamic_slice(view, (position[s] // NEED, position[s] % NEED * (width // sub), 0, 0),
                              (1, width // sub, sub, tile_size)).reshape(width, tile_size)
            for s in range(off_count)])
        near = batched_tile_dot(x, grm_tiles[:row_tiles])
        far = batched_tile_dot(picked, grm_tiles[row_tiles:])
        return near + jnp.sum(weight[:, :, None, None] * far[:, None], axis=0)

    def colsum(x):
        return jnp.sum(x, axis=(0, 2))

    geno_all = lax.all_gather(genotypes, "var", axis=0, tiled=True)
    first = v * cols_here
    a_out = first // genes
    g0 = first % genes
    geno_sub = jnp.stack(
        [to_tiles(lax.dynamic_slice_in_dim(geno_all, a * genes + g0, cols_here, 0))
         for a in range(VARS_GENE)]
    )

    def chunk(g, geno_sub):
        z0 = g / precond
        tiles0, sums0 = exchange(z0, colsum(g * z0)[None])
        rz0 = sums0[0]
        kz0 = kprod(z0, tiles0)
        image0 = tau0 * z0 + tau1 * kz0
        w = image0 / precond
        p0_local = jnp.sum(geno_sub * z0[None], axis=(1, 3))
        extra1 = jnp.concatenate([colsum(z0 * image0)[None], p0_local], axis=0)
        tiles1, sums1 = exchange(w, extra1, by_concat=True)
        dad0 = sums1[0]
        p0 = sums1[1:]
        alpha0 = rz0 / dad0
        resid1 = g - alpha0[None, :, None] * image0
        z1 = resid1 / precond
        kw = kprod(w, tiles1)
        kz1 = kz0 - alpha0[None, :, None] * kw
        az1 = tau0 * z1 + tau1 * kz1
        red_local = jnp.concatenate(
            [colsum(resid1 * z1)[None], colsum(z1 * az1)[None],
             colsum(z1 * image0 + z0 * az1)[None], jnp.sum(geno_sub * z1[None], axis=(1, 3))],
            axis=0,
        )
        lead = (me == 0).astype(jnp.float32)
        payload = jnp.concatenate(
            [red_local, lead * rz0[None], lead * dad0[None], lead * p0], axis=0)
        spread = jnp.broadcast_to(payload[None], (peers * nvar,) + payload.shape)
        got = lax.all_to_all(spread, ("ind", "var"), split_axis=0, concat_axis=0, tiled=True)
        tot = jnp.sum(got.reshape((peers, nvar) + payload.shape), axis=0)
        nv = VARS_GENE
        rz1_all = tot[:, 0]
        rz0_all = tot[:, 3 + nv]
        dad0_all = tot[:, 4 + nv]
        p0_all = tot[:, 5 + nv:]
        p1_all = tot[:, 3:3 + nv]
        alpha0_all = rz0_all / dad0_all
        beta_all = rz1_all / rz0_all
        dad1_all = tot[:, 1] + beta_all * (tot[:, 2] + beta_all * dad0_all)
        alpha1_all = rz1_all / dad1_all
        mine = lambda t: lax.dynamic_index_in_dim(t, v, 0, keepdims=False)
        beta = mine(beta_all)
        alpha1 = mine(alpha1_all)
        dir1 = z1 + beta[None, :, None] * z0
        sol = alpha0[None, :, None] * z0 + alpha1[None, :, None] * dir1
        part = alpha0_all[:, None] * p0_all + alpha1_all[:, None] * (p1_all + beta_all[:, None] * p0_all)
        return sol, part

    g_all = to_tiles(genotypes)
    width = cols_here // CHUNKS
    outs = [chunk(g_all[:, k * width:(k + 1) * width], geno_sub[:, :, k * width:(k + 1) * width])
            for k in range(CHUNKS)]
    solution = jnp.concatenate([o[0] for o in outs], axis=1)
    gram_part = jnp.concatenate([o[1] for o in outs], axis=2)
    full = jnp.transpose(gram_part, (1, 0, 2)).reshape(VARS_GENE, ncol)
    gram_cols = lax.dynamic_index_in_dim(full, a_out, 0, keepdims=False)
    gram_cols = lax.dynamic_slice_in_dim(gram_cols.reshape(VARS_GENE, genes), g0, cols_here, 1)
    gene_gram = jnp.transpose(gram_cols) / total_ind
    return (from_tiles(solution), gene_gram)


def solution(mesh):
    placed = (P("var", "ind"), P(), P("ind", None, None), P("ind"), P("ind"), P("ind"))
    return jax.shard_map(
        local,
        mesh=mesh,
        in_specs=placed,
        out_specs=(P("var", "ind"), P("var", None)),
        check_vma=False,
    )
```

```python
import jax
import jax.numpy as jnp
from jax import lax
from jax.sharding import PartitionSpec as P

VARS_GENE = 4
NEED = 2
PAD_ROWS = 8
CHUNKS = 1


def split2(x):
    hi = lax.reduce_precision(x, exponent_bits=8, mantissa_bits=7)
    lo = x - hi
    return hi.astype(jnp.bfloat16), lo.astype(jnp.bfloat16)


def batched_tile_dot(lhs, tiles):
    cols = lhs.shape[1]
    parts = jnp.concatenate(split2(lhs), axis=1)
    prod = lax.dot_general(
        parts, tiles, (((2,), (2,)), ((0,), (0,))), preferred_element_type=jnp.float32
    )
    return prod[:, :cols] + prod[:, cols:]


def local(genotypes, variance_comp, grm_tiles, tile_rows, tile_cols, tile_live):
    cols_here, rows_here = genotypes.shape
    tile_size = grm_tiles.shape[1]
    slot_count = grm_tiles.shape[0]
    row_tiles = rows_here // tile_size
    off_count = slot_count - row_tiles
    me = lax.axis_index("ind")
    peers = lax.axis_size("ind")
    v = lax.axis_index("var")
    nvar = lax.axis_size("var")
    ncol = cols_here * nvar
    genes = ncol // VARS_GENE
    total_ind = peers * rows_here
    tau0 = variance_comp[0]
    tau1 = variance_comp[1]
    live = tile_live[0]

    eye = jnp.arange(tile_size)[:, None] == jnp.arange(tile_size)[None, :]
    diag_values = jnp.sum(
        jnp.where(eye[None], grm_tiles[:row_tiles].astype(jnp.float32), 0.0), axis=2
    )
    precond = (tau0 + tau1 * diag_values)[:, None, :]
    off_rows = tile_rows[row_tiles:]
    off_cols = tile_cols[row_tiles:]
    live_mask = (jnp.arange(row_tiles, slot_count, dtype=jnp.int32) < live).astype(jnp.float32)
    weight = (off_rows[:, None] == jnp.arange(row_tiles, dtype=jnp.int32)[None, :]).astype(jnp.float32)
    weight = weight * live_mask[:, None]
    position = off_cols // row_tiles * NEED + (off_cols % row_tiles - me) % row_tiles
    position = jnp.clip(position, 0, peers * NEED - 1)

    def to_tiles(x):
        return jnp.transpose(x.reshape(cols_here, row_tiles, tile_size), (1, 0, 2))

    def from_tiles(x):
        return jnp.transpose(x, (1, 0, 2)).reshape(cols_here, rows_here)

    def exchange(x, extra, by_concat=False):
        width = x.shape[1]
        flat = extra.reshape(-1)
        flat = jnp.pad(flat, (0, PAD_ROWS * tile_size - flat.shape[0]))
        if by_concat:
            rows = []
            for p in range(peers):
                rows += [x[(p + t) % row_tiles] for t in range(NEED)]
                rows.append(flat.reshape(PAD_ROWS, tile_size))
            pieces = jnp.concatenate(rows, axis=0).reshape(peers, -1, tile_size)
        else:
            rolled = jnp.stack([jnp.roll(x, -t, axis=0) for t in range(NEED)], axis=1)
            rolled = rolled.reshape(row_tiles, NEED * width, tile_size)
            pieces = jnp.tile(rolled, (peers // row_tiles, 1, 1))
            side = jnp.broadcast_to(flat.reshape(1, PAD_ROWS, tile_size), (peers, PAD_ROWS, tile_size))
            pieces = jnp.concatenate([pieces, side], axis=1)
        arrived = lax.all_to_all(pieces, "ind", split_axis=0, concat_axis=0, tiled=True)
        tiles_in = arrived[:, :NEED * width].reshape(peers * NEED, width, tile_size)
        sums = jnp.sum(arrived[:, NEED * width:].reshape(peers, -1)[:, :extra.size], axis=0)
        return tiles_in, sums.reshape(extra.shape)

    def kprod(x, arrived):
        width = x.shape[1]
        picked = jnp.stack([lax.dynamic_index_in_dim(arrived, position[s], 0, keepdims=False)
                            for s in range(off_count)])
        near = batched_tile_dot(x, grm_tiles[:row_tiles])
        far = batched_tile_dot(picked, grm_tiles[row_tiles:])
        return near + jnp.sum(weight[:, :, None, None] * far[:, None], axis=0)

    def colsum(x):
        return jnp.sum(x, axis=(0, 2))

    geno_all = lax.all_gather(genotypes, "var", axis=0, tiled=True)
    first = v * cols_here
    a_out = first // genes
    g0 = first % genes
    geno_sub = jnp.stack(
        [to_tiles(lax.dynamic_slice_in_dim(geno_all, a * genes + g0, cols_here, 0))
         for a in range(VARS_GENE)]
    )

    def chunk(g, geno_sub):
        z0 = g / precond
        tiles0, sums0 = exchange(z0, colsum(g * z0)[None])
        rz0 = sums0[0]
        kz0 = kprod(z0, tiles0)
        image0 = tau0 * z0 + tau1 * kz0
        w = image0 / precond
        p0_local = jnp.sum(geno_sub * z0[None], axis=(1, 3))
        extra1 = jnp.concatenate([colsum(z0 * image0)[None], p0_local], axis=0)
        tiles1, sums1 = exchange(w, extra1, by_concat=True)
        dad0 = sums1[0]
        p0 = sums1[1:]
        alpha0 = rz0 / dad0
        resid1 = g - alpha0[None, :, None] * image0
        z1 = resid1 / precond
        kw = kprod(w, tiles1)
        kz1 = kz0 - alpha0[None, :, None] * kw
        az1 = tau0 * z1 + tau1 * kz1
        pw_local = jnp.sum(geno_sub * w[None], axis=(1, 3))
        p1_local = p0_local - alpha0[None] * pw_local
        red_local = jnp.concatenate(
            [colsum(resid1 * z1)[None], colsum(z1 * az1)[None],
             colsum(z1 * image0 + z0 * az1)[None], p1_local],
            axis=0,
        )
        z0_rows = from_tiles(z0)
        z1_rows = from_tiles(z1)
        lead = (me == 0).astype(jnp.float32)
        payload = jnp.concatenate(
            [red_local, lead * rz0[None], lead * dad0[None], lead * p0], axis=0)
        spread = jnp.broadcast_to(payload[None], (peers * nvar,) + payload.shape)
        got = lax.all_to_all(spread, ("ind", "var"), split_axis=0, concat_axis=0, tiled=True)
        tot = jnp.sum(got.reshape((peers, nvar) + payload.shape), axis=0)
        nv = VARS_GENE
        rz1_all = tot[:, 0]
        rz0_all = tot[:, 3 + nv]
        dad0_all = tot[:, 4 + nv]
        p0_all = tot[:, 5 + nv:]
        p1_all = tot[:, 3:3 + nv]
        alpha0_all = rz0_all / dad0_all
        beta_all = rz1_all / rz0_all
        dad1_all = tot[:, 1] + beta_all * (tot[:, 2] + beta_all * dad0_all)
        alpha1_all = rz1_all / dad1_all
        mine = lambda t: lax.dynamic_index_in_dim(t, v, 0, keepdims=False)
        beta = mine(beta_all)
        alpha1 = mine(alpha1_all)
        dir1 = z1_rows + beta[:, None] * z0_rows
        sol = alpha0[:, None] * z0_rows + alpha1[:, None] * dir1
        part = alpha0_all[:, None] * p0_all + alpha1_all[:, None] * (p1_all + beta_all[:, None] * p0_all)
        return sol, part

    g_all = to_tiles(genotypes)
    width = cols_here // CHUNKS
    outs = [chunk(g_all[:, k * width:(k + 1) * width], geno_sub[:, :, k * width:(k + 1) * width])
            for k in range(CHUNKS)]
    solution = jnp.concatenate([o[0] for o in outs], axis=0)
    gram_part = jnp.concatenate([o[1] for o in outs], axis=2)
    full = jnp.transpose(gram_part, (1, 0, 2)).reshape(VARS_GENE, ncol)
    gram_cols = lax.dynamic_index_in_dim(full, a_out, 0, keepdims=False)
    gram_cols = lax.dynamic_slice_in_dim(gram_cols.reshape(VARS_GENE, genes), g0, cols_here, 1)
    gene_gram = jnp.transpose(gram_cols) / total_ind
    return (solution, gene_gram)


def solution(mesh):
    placed = (P("var", "ind"), P(), P("ind", None, None), P("ind"), P("ind"), P("ind"))
    return jax.shard_map(
        local,
        mesh=mesh,
        in_specs=placed,
        out_specs=(P("var", "ind"), P("var", None)),
        check_vma=False,
    )
```

```python
import jax
import jax.numpy as jnp
from jax import lax
from jax.sharding import PartitionSpec as P
from jax.experimental import pallas as pl
from jax.experimental.pallas import tpu as pltpu

VARS_GENE = 4
NEED = 2
PAD_ROWS = 8
CHUNKS = 1


def split2(x):
    hi = lax.reduce_precision(x, exponent_bits=8, mantissa_bits=7)
    lo = x - hi
    return hi.astype(jnp.bfloat16), lo.astype(jnp.bfloat16)


def batched_tile_dot(lhs, tiles):
    cols = lhs.shape[1]
    parts = jnp.concatenate(split2(lhs), axis=1)
    prod = lax.dot_general(
        parts, tiles, (((2,), (2,)), ((0,), (0,))), preferred_element_type=jnp.float32
    )
    return prod[:, :cols] + prod[:, cols:]


def diag_kernel(t_ref, o_ref):
    tile = t_ref[0].astype(jnp.float32)
    size = tile.shape[0]
    rows = lax.broadcasted_iota(jnp.int32, (size, size), 0)
    cols = lax.broadcasted_iota(jnp.int32, (size, size), 1)
    o_ref[0] = jnp.sum(jnp.where(rows == cols, tile, 0.0), axis=0, keepdims=True)


def tile_diagonals(tiles, count):
    size = tiles.shape[1]
    out = pl.pallas_call(
        diag_kernel,
        grid=(count,),
        in_specs=[pl.BlockSpec((1, size, size), lambda i: (i, 0, 0))],
        out_specs=pl.BlockSpec((1, 1, size), lambda i: (i, 0, 0)),
        out_shape=jax.ShapeDtypeStruct((count, 1, size), jnp.float32),
        cost_estimate=pl.CostEstimate(
            flops=count * size * size, transcendentals=0,
            bytes_accessed=count * size * size * 2 + count * size * 4),
    )(tiles)
    return out.reshape(count, size)


def local(genotypes, variance_comp, grm_tiles, tile_rows, tile_cols, tile_live):
    cols_here, rows_here = genotypes.shape
    tile_size = grm_tiles.shape[1]
    slot_count = grm_tiles.shape[0]
    row_tiles = rows_here // tile_size
    off_count = slot_count - row_tiles
    me = lax.axis_index("ind")
    peers = lax.axis_size("ind")
    v = lax.axis_index("var")
    nvar = lax.axis_size("var")
    ncol = cols_here * nvar
    genes = ncol // VARS_GENE
    total_ind = peers * rows_here
    tau0 = variance_comp[0]
    tau1 = variance_comp[1]
    live = tile_live[0]

    diag_values = tile_diagonals(grm_tiles, row_tiles)
    precond = (tau0 + tau1 * diag_values)[:, None, :]
    off_rows = tile_rows[row_tiles:]
    off_cols = tile_cols[row_tiles:]
    live_mask = (jnp.arange(row_tiles, slot_count, dtype=jnp.int32) < live).astype(jnp.float32)
    weight = (off_rows[:, None] == jnp.arange(row_tiles, dtype=jnp.int32)[None, :]).astype(jnp.float32)
    weight = weight * live_mask[:, None]
    position = off_cols // row_tiles * NEED + (off_cols % row_tiles - me) % row_tiles
    position = jnp.clip(position, 0, peers * NEED - 1)

    def to_tiles(x):
        return jnp.transpose(x.reshape(cols_here, row_tiles, tile_size), (1, 0, 2))

    def from_tiles(x):
        return jnp.transpose(x, (1, 0, 2)).reshape(cols_here, rows_here)

    def exchange(x, extra, by_concat=False):
        width = x.shape[1]
        flat = extra.reshape(-1)
        flat = jnp.pad(flat, (0, PAD_ROWS * tile_size - flat.shape[0]))
        if by_concat:
            rows = []
            for p in range(peers):
                rows += [x[(p + t) % row_tiles] for t in range(NEED)]
                rows.append(flat.reshape(PAD_ROWS, tile_size))
            pieces = jnp.concatenate(rows, axis=0).reshape(peers, -1, tile_size)
        else:
            rolled = jnp.stack([jnp.roll(x, -t, axis=0) for t in range(NEED)], axis=1)
            rolled = rolled.reshape(row_tiles, NEED * width, tile_size)
            pieces = jnp.tile(rolled, (peers // row_tiles, 1, 1))
            side = jnp.broadcast_to(flat.reshape(1, PAD_ROWS, tile_size), (peers, PAD_ROWS, tile_size))
            pieces = jnp.concatenate([pieces, side], axis=1)
        arrived = lax.all_to_all(pieces, "ind", split_axis=0, concat_axis=0, tiled=True)
        tiles_in = arrived[:, :NEED * width].reshape(peers * NEED, width, tile_size)
        sums = jnp.sum(arrived[:, NEED * width:].reshape(peers, -1)[:, :extra.size], axis=0)
        return tiles_in, sums.reshape(extra.shape)

    def kprod(x, arrived):
        width = x.shape[1]
        picked = jnp.stack([lax.dynamic_index_in_dim(arrived, position[s], 0, keepdims=False)
                            for s in range(off_count)])
        near = batched_tile_dot(x, grm_tiles[:row_tiles])
        far = batched_tile_dot(picked, grm_tiles[row_tiles:])
        return near + jnp.sum(weight[:, :, None, None] * far[:, None], axis=0)

    def colsum(x):
        return jnp.sum(x, axis=(0, 2))

    geno_all = lax.all_gather(genotypes, "var", axis=0, tiled=True)
    first = v * cols_here
    a_out = first // genes
    g0 = first % genes
    geno_sub = jnp.stack(
        [to_tiles(lax.dynamic_slice_in_dim(geno_all, a * genes + g0, cols_here, 0))
         for a in range(VARS_GENE)]
    )

    def chunk(g, geno_sub):
        z0 = g / precond
        tiles0, sums0 = exchange(z0, colsum(g * z0)[None])
        rz0 = sums0[0]
        kz0 = kprod(z0, tiles0)
        image0 = tau0 * z0 + tau1 * kz0
        w = image0 / precond
        p0_local = jnp.sum(geno_sub * z0[None], axis=(1, 3))
        extra1 = jnp.concatenate([colsum(z0 * image0)[None], p0_local], axis=0)
        tiles1, sums1 = exchange(w, extra1, by_concat=True)
        dad0 = sums1[0]
        p0 = sums1[1:]
        alpha0 = rz0 / dad0
        resid1 = g - alpha0[None, :, None] * image0
        z1 = resid1 / precond
        kw = kprod(w, tiles1)
        kz1 = kz0 - alpha0[None, :, None] * kw
        az1 = tau0 * z1 + tau1 * kz1
        red_local = jnp.concatenate(
            [colsum(resid1 * z1)[None], colsum(z1 * az1)[None],
             colsum(z1 * image0 + z0 * az1)[None], jnp.sum(geno_sub * z1[None], axis=(1, 3))],
            axis=0,
        )
        lead = (me == 0).astype(jnp.float32)
        payload = jnp.concatenate(
            [red_local, lead * rz0[None], lead * dad0[None], lead * p0], axis=0)
        spread = jnp.broadcast_to(payload[None], (peers * nvar,) + payload.shape)
        got = lax.all_to_all(spread, ("ind", "var"), split_axis=0, concat_axis=0, tiled=True)
        tot = jnp.sum(got.reshape((peers, nvar) + payload.shape), axis=0)
        nv = VARS_GENE
        rz1_all = tot[:, 0]
        rz0_all = tot[:, 3 + nv]
        dad0_all = tot[:, 4 + nv]
        p0_all = tot[:, 5 + nv:]
        p1_all = tot[:, 3:3 + nv]
        alpha0_all = rz0_all / dad0_all
        beta_all = rz1_all / rz0_all
        dad1_all = tot[:, 1] + beta_all * (tot[:, 2] + beta_all * dad0_all)
        alpha1_all = rz1_all / dad1_all
        mine = lambda t: lax.dynamic_index_in_dim(t, v, 0, keepdims=False)
        beta = mine(beta_all)
        alpha1 = mine(alpha1_all)
        dir1 = z1 + beta[None, :, None] * z0
        sol = alpha0[None, :, None] * z0 + alpha1[None, :, None] * dir1
        part = alpha0_all[:, None] * p0_all + alpha1_all[:, None] * (p1_all + beta_all[:, None] * p0_all)
        return sol, part

    g_all = to_tiles(genotypes)
    width = cols_here // CHUNKS
    outs = [chunk(g_all[:, k * width:(k + 1) * width], geno_sub[:, :, k * width:(k + 1) * width])
            for k in range(CHUNKS)]
    solution = jnp.concatenate([o[0] for o in outs], axis=1)
    gram_part = jnp.concatenate([o[1] for o in outs], axis=2)
    full = jnp.transpose(gram_part, (1, 0, 2)).reshape(VARS_GENE, ncol)
    gram_cols = lax.dynamic_index_in_dim(full, a_out, 0, keepdims=False)
    gram_cols = lax.dynamic_slice_in_dim(gram_cols.reshape(VARS_GENE, genes), g0, cols_here, 1)
    gene_gram = jnp.transpose(gram_cols) / total_ind
    return (from_tiles(solution), gene_gram)


def solution(mesh):
    placed = (P("var", "ind"), P(), P("ind", None, None), P("ind"), P("ind"), P("ind"))
    return jax.shard_map(
        local,
        mesh=mesh,
        in_specs=placed,
        out_specs=(P("var", "ind"), P("var", None)),
        check_vma=False,
    )
```

```python
import jax
import jax.numpy as jnp
from jax import lax
from jax.sharding import PartitionSpec as P

VARS_GENE = 4
NEED = 2
PAD_ROWS = 8
CHUNKS = 1


def split2(x):
    hi = lax.reduce_precision(x, exponent_bits=8, mantissa_bits=7)
    lo = x - hi
    return hi.astype(jnp.bfloat16), lo.astype(jnp.bfloat16)


def batched_tile_dot(lhs, tiles):
    cols = lhs.shape[1]
    parts = jnp.concatenate(split2(lhs), axis=1)
    prod = lax.dot_general(
        parts, tiles, (((2,), (2,)), ((0,), (0,))), preferred_element_type=jnp.float32
    )
    return prod[:, :cols] + prod[:, cols:]


def local(genotypes, variance_comp, grm_tiles, tile_rows, tile_cols, tile_live):
    cols_here, rows_here = genotypes.shape
    tile_size = grm_tiles.shape[1]
    slot_count = grm_tiles.shape[0]
    row_tiles = rows_here // tile_size
    off_count = slot_count - row_tiles
    me = lax.axis_index("ind")
    peers = lax.axis_size("ind")
    v = lax.axis_index("var")
    nvar = lax.axis_size("var")
    ncol = cols_here * nvar
    genes = ncol // VARS_GENE
    total_ind = peers * rows_here
    tau0 = variance_comp[0]
    tau1 = variance_comp[1]
    live = tile_live[0]

    eye = jnp.arange(tile_size)[:, None] == jnp.arange(tile_size)[None, :]
    diag_values = jnp.sum(
        jnp.where(eye[None], grm_tiles[:row_tiles].astype(jnp.float32), 0.0), axis=2
    )
    precond = (tau0 + tau1 * diag_values)[:, None, :]
    off_rows = tile_rows[row_tiles:]
    off_cols = tile_cols[row_tiles:]
    live_mask = (jnp.arange(row_tiles, slot_count, dtype=jnp.int32) < live).astype(jnp.float32)
    weight = (off_rows[:, None] == jnp.arange(row_tiles, dtype=jnp.int32)[None, :]).astype(jnp.float32)
    weight = weight * live_mask[:, None]
    position = off_cols // row_tiles * NEED + (off_cols % row_tiles - me) % row_tiles
    position = jnp.clip(position, 0, peers * NEED - 1)

    def to_tiles(x):
        return jnp.transpose(x.reshape(cols_here, row_tiles, tile_size), (1, 0, 2))

    def from_tiles(x):
        return jnp.transpose(x, (1, 0, 2)).reshape(cols_here, rows_here)

    def exchange(x, extra, by_concat=False):
        width = x.shape[1]
        if by_concat:
            rows = []
            for p in range(peers):
                rows += [x[(p + t) % row_tiles] for t in range(NEED)]
            pieces = jnp.concatenate(rows, axis=0).reshape(peers * NEED, width, tile_size)
            arrived = lax.all_to_all(pieces, "ind", split_axis=0, concat_axis=0, tiled=True)
            return arrived, None
        flat = extra.reshape(-1)
        flat = jnp.pad(flat, (0, PAD_ROWS * tile_size - flat.shape[0]))
        if by_concat:
            pieces = None
        else:
            rolled = jnp.stack([jnp.roll(x, -t, axis=0) for t in range(NEED)], axis=1)
            rolled = rolled.reshape(row_tiles, NEED * width, tile_size)
            pieces = jnp.tile(rolled, (peers // row_tiles, 1, 1))
            side = jnp.broadcast_to(flat.reshape(1, PAD_ROWS, tile_size), (peers, PAD_ROWS, tile_size))
            pieces = jnp.concatenate([pieces, side], axis=1)
        arrived = lax.all_to_all(pieces, "ind", split_axis=0, concat_axis=0, tiled=True)
        tiles_in = arrived[:, :NEED * width].reshape(peers * NEED, width, tile_size)
        sums = jnp.sum(arrived[:, NEED * width:].reshape(peers, -1)[:, :extra.size], axis=0)
        return tiles_in, sums.reshape(extra.shape)

    def kprod(x, arrived, gather=False):
        width = x.shape[1]
        if gather:
            picked = jnp.take(arrived, position, axis=0, mode="clip")
        else:
            picked = jnp.stack([lax.dynamic_index_in_dim(arrived, position[s], 0, keepdims=False)
                                for s in range(off_count)])
        near = batched_tile_dot(x, grm_tiles[:row_tiles])
        far = batched_tile_dot(picked, grm_tiles[row_tiles:])
        return near + jnp.sum(weight[:, :, None, None] * far[:, None], axis=0)

    def colsum(x):
        return jnp.sum(x, axis=(0, 2))

    geno_all = lax.all_gather(genotypes, "var", axis=0, tiled=True)
    first = v * cols_here
    a_out = first // genes
    g0 = first % genes
    geno_sub = jnp.stack(
        [to_tiles(lax.dynamic_slice_in_dim(geno_all, a * genes + g0, cols_here, 0))
         for a in range(VARS_GENE)]
    )

    def chunk(g, geno_sub):
        z0 = g / precond
        tiles0, sums0 = exchange(z0, colsum(g * z0)[None])
        rz0 = sums0[0]
        kz0 = kprod(z0, tiles0)
        image0 = tau0 * z0 + tau1 * kz0
        w = image0 / precond
        p0_local = jnp.sum(geno_sub * z0[None], axis=(1, 3))
        dad0 = lax.psum(colsum(z0 * image0), "ind")
        tiles1, _ = exchange(w, None, by_concat=True)
        alpha0 = rz0 / dad0
        resid1 = g - alpha0[None, :, None] * image0
        z1 = resid1 / precond
        kw = kprod(w, tiles1, gather=True)
        kz1 = kz0 - alpha0[None, :, None] * kw
        az1 = tau0 * z1 + tau1 * kz1
        red_local = jnp.concatenate(
            [colsum(resid1 * z1)[None], colsum(z1 * az1)[None],
             colsum(z1 * image0 + z0 * az1)[None], jnp.sum(geno_sub * z1[None], axis=(1, 3))],
            axis=0,
        )
        lead = (me == 0).astype(jnp.float32)
        payload = jnp.concatenate(
            [red_local, lead * rz0[None], lead * dad0[None], p0_local], axis=0)
        spread = jnp.broadcast_to(payload[None], (peers * nvar,) + payload.shape)
        got = lax.all_to_all(spread, ("ind", "var"), split_axis=0, concat_axis=0, tiled=True)
        tot = jnp.sum(got.reshape((peers, nvar) + payload.shape), axis=0)
        nv = VARS_GENE
        rz1_all = tot[:, 0]
        rz0_all = tot[:, 3 + nv]
        dad0_all = tot[:, 4 + nv]
        p0_all = tot[:, 5 + nv:]
        p1_all = tot[:, 3:3 + nv]
        alpha0_all = rz0_all / dad0_all
        beta_all = rz1_all / rz0_all
        dad1_all = tot[:, 1] + beta_all * (tot[:, 2] + beta_all * dad0_all)
        alpha1_all = rz1_all / dad1_all
        mine = lambda t: lax.dynamic_index_in_dim(t, v, 0, keepdims=False)
        beta = mine(beta_all)
        alpha1 = mine(alpha1_all)
        dir1 = z1 + beta[None, :, None] * z0
        sol = alpha0[None, :, None] * z0 + alpha1[None, :, None] * dir1
        part = alpha0_all[:, None] * p0_all + alpha1_all[:, None] * (p1_all + beta_all[:, None] * p0_all)
        return sol, part

    g_all = to_tiles(genotypes)
    width = cols_here // CHUNKS
    outs = [chunk(g_all[:, k * width:(k + 1) * width], geno_sub[:, :, k * width:(k + 1) * width])
            for k in range(CHUNKS)]
    solution = jnp.concatenate([o[0] for o in outs], axis=1)
    gram_part = jnp.concatenate([o[1] for o in outs], axis=2)
    full = jnp.transpose(gram_part, (1, 0, 2)).reshape(VARS_GENE, ncol)
    gram_cols = lax.dynamic_index_in_dim(full, a_out, 0, keepdims=False)
    gram_cols = lax.dynamic_slice_in_dim(gram_cols.reshape(VARS_GENE, genes), g0, cols_here, 1)
    gene_gram = jnp.transpose(gram_cols) / total_ind
    return (from_tiles(solution), gene_gram)


def solution(mesh):
    placed = (P("var", "ind"), P(), P("ind", None, None), P("ind"), P("ind"), P("ind"))
    return jax.shard_map(
        local,
        mesh=mesh,
        in_specs=placed,
        out_specs=(P("var", "ind"), P("var", None)),
        check_vma=False,
    )
```

```python
import jax
import jax.numpy as jnp
from jax import lax
from jax.sharding import PartitionSpec as P

VARS_GENE = 4
NEED = 2
PAD_ROWS = 8
CHUNKS = 1


def split2(x):
    hi = lax.reduce_precision(x, exponent_bits=8, mantissa_bits=7)
    lo = x - hi
    return hi.astype(jnp.bfloat16), lo.astype(jnp.bfloat16)


def batched_tile_dot(lhs, tiles):
    cols = lhs.shape[1]
    parts = jnp.concatenate(split2(lhs), axis=1)
    prod = lax.dot_general(
        parts, tiles, (((2,), (2,)), ((0,), (0,))), preferred_element_type=jnp.float32
    )
    return prod[:, :cols] + prod[:, cols:]


def local(genotypes, variance_comp, grm_tiles, tile_rows, tile_cols, tile_live):
    cols_here, rows_here = genotypes.shape
    tile_size = grm_tiles.shape[1]
    slot_count = grm_tiles.shape[0]
    row_tiles = rows_here // tile_size
    off_count = slot_count - row_tiles
    me = lax.axis_index("ind")
    peers = lax.axis_size("ind")
    v = lax.axis_index("var")
    nvar = lax.axis_size("var")
    ncol = cols_here * nvar
    genes = ncol // VARS_GENE
    total_ind = peers * rows_here
    tau0 = variance_comp[0]
    tau1 = variance_comp[1]
    live = tile_live[0]

    eye = jnp.arange(tile_size)[:, None] == jnp.arange(tile_size)[None, :]
    diag_values = jnp.sum(
        jnp.where(eye[None], grm_tiles[:row_tiles].astype(jnp.float32), 0.0), axis=2
    )
    precond = (tau0 + tau1 * diag_values)[:, None, :]
    off_rows = tile_rows[row_tiles:]
    off_cols = tile_cols[row_tiles:]
    live_mask = (jnp.arange(row_tiles, slot_count, dtype=jnp.int32) < live).astype(jnp.float32)
    weight = (off_rows[:, None] == jnp.arange(row_tiles, dtype=jnp.int32)[None, :]).astype(jnp.float32)
    weight = weight * live_mask[:, None]
    position = off_cols // row_tiles * NEED + (off_cols % row_tiles - me) % row_tiles
    position = jnp.clip(position, 0, peers * NEED - 1)

    def to_tiles(x):
        return jnp.transpose(x.reshape(cols_here, row_tiles, tile_size), (1, 0, 2))

    def from_tiles(x):
        return jnp.transpose(x, (1, 0, 2)).reshape(cols_here, rows_here)

    def exchange(x, extra, by_concat=False):
        width = x.shape[1]
        flat = extra.reshape(-1)
        flat = jnp.pad(flat, (0, PAD_ROWS * tile_size - flat.shape[0]))
        if by_concat:
            rows = []
            for p in range(peers):
                rows += [x[(p + t) % row_tiles] for t in range(NEED)]
                rows.append(flat.reshape(PAD_ROWS, tile_size))
            pieces = jnp.concatenate(rows, axis=0).reshape(peers, -1, tile_size)
        else:
            rolled = jnp.stack([jnp.roll(x, -t, axis=0) for t in range(NEED)], axis=1)
            rolled = rolled.reshape(row_tiles, NEED * width, tile_size)
            pieces = jnp.tile(rolled, (peers // row_tiles, 1, 1))
            side = jnp.broadcast_to(flat.reshape(1, PAD_ROWS, tile_size), (peers, PAD_ROWS, tile_size))
            pieces = jnp.concatenate([pieces, side], axis=1)
        arrived = lax.all_to_all(pieces, "ind", split_axis=0, concat_axis=0, tiled=True)
        tiles_in = arrived[:, :NEED * width].reshape(peers * NEED, width, tile_size)
        sums = jnp.sum(arrived[:, NEED * width:].reshape(peers, -1)[:, :extra.size], axis=0)
        return tiles_in, sums.reshape(extra.shape)

    def kprod(x, arrived):
        width = x.shape[1]
        picked = jnp.stack([lax.dynamic_index_in_dim(arrived, position[s], 0, keepdims=False)
                            for s in range(off_count)])
        near = batched_tile_dot(x, grm_tiles[:row_tiles])
        far = batched_tile_dot(picked, grm_tiles[row_tiles:])
        return near + jnp.sum(weight[:, :, None, None] * far[:, None], axis=0)

    def colsum(x):
        return jnp.sum(x, axis=(0, 2))

    parts = [genotypes] + [
        lax.ppermute(genotypes, "var", [(j, (j + k) % nvar) for j in range(nvar)])
        for k in range(1, nvar)]
    parts = jnp.stack(parts)
    order = (v - jnp.arange(nvar, dtype=jnp.int32)) % nvar
    geno_all = jnp.take(parts, order, axis=0, mode="clip").reshape(ncol, rows_here)
    first = v * cols_here
    a_out = first // genes
    g0 = first % genes
    geno_sub = jnp.stack(
        [to_tiles(lax.dynamic_slice_in_dim(geno_all, a * genes + g0, cols_here, 0))
         for a in range(VARS_GENE)]
    )

    def chunk(g, geno_sub):
        z0 = g / precond
        tiles0, sums0 = exchange(z0, colsum(g * z0)[None])
        rz0 = sums0[0]
        kz0 = kprod(z0, tiles0)
        image0 = tau0 * z0 + tau1 * kz0
        w = image0 / precond
        p0_local = jnp.sum(geno_sub * z0[None], axis=(1, 3))
        extra1 = jnp.concatenate([colsum(z0 * image0)[None], p0_local], axis=0)
        tiles1, sums1 = exchange(w, extra1, by_concat=True)
        dad0 = sums1[0]
        p0 = sums1[1:]
        alpha0 = rz0 / dad0
        resid1 = g - alpha0[None, :, None] * image0
        z1 = resid1 / precond
        kw = kprod(w, tiles1)
        kz1 = kz0 - alpha0[None, :, None] * kw
        az1 = tau0 * z1 + tau1 * kz1
        red_local = jnp.concatenate(
            [colsum(resid1 * z1)[None], colsum(z1 * az1)[None],
             colsum(z1 * image0 + z0 * az1)[None], jnp.sum(geno_sub * z1[None], axis=(1, 3))],
            axis=0,
        )
        lead = (me == 0).astype(jnp.float32)
        payload = jnp.concatenate(
            [red_local, lead * rz0[None], lead * dad0[None], lead * p0], axis=0)
        spread = jnp.broadcast_to(payload[None], (peers * nvar,) + payload.shape)
        got = lax.all_to_all(spread, ("ind", "var"), split_axis=0, concat_axis=0, tiled=True)
        tot = jnp.sum(got.reshape((peers, nvar) + payload.shape), axis=0)
        nv = VARS_GENE
        rz1_all = tot[:, 0]
        rz0_all = tot[:, 3 + nv]
        dad0_all = tot[:, 4 + nv]
        p0_all = tot[:, 5 + nv:]
        p1_all = tot[:, 3:3 + nv]
        alpha0_all = rz0_all / dad0_all
        beta_all = rz1_all / rz0_all
        dad1_all = tot[:, 1] + beta_all * (tot[:, 2] + beta_all * dad0_all)
        alpha1_all = rz1_all / dad1_all
        mine = lambda t: lax.dynamic_index_in_dim(t, v, 0, keepdims=False)
        beta = mine(beta_all)
        alpha1 = mine(alpha1_all)
        dir1 = z1 + beta[None, :, None] * z0
        sol = alpha0[None, :, None] * z0 + alpha1[None, :, None] * dir1
        part = alpha0_all[:, None] * p0_all + alpha1_all[:, None] * (p1_all + beta_all[:, None] * p0_all)
        return sol, part

    g_all = to_tiles(genotypes)
    width = cols_here // CHUNKS
    outs = [chunk(g_all[:, k * width:(k + 1) * width], geno_sub[:, :, k * width:(k + 1) * width])
            for k in range(CHUNKS)]
    solution = jnp.concatenate([o[0] for o in outs], axis=1)
    gram_part = jnp.concatenate([o[1] for o in outs], axis=2)
    full = jnp.transpose(gram_part, (1, 0, 2)).reshape(VARS_GENE, ncol)
    gram_cols = lax.dynamic_index_in_dim(full, a_out, 0, keepdims=False)
    gram_cols = lax.dynamic_slice_in_dim(gram_cols.reshape(VARS_GENE, genes), g0, cols_here, 1)
    gene_gram = jnp.transpose(gram_cols) / total_ind
    return (from_tiles(solution), gene_gram)


def solution(mesh):
    placed = (P("var", "ind"), P(), P("ind", None, None), P("ind"), P("ind"), P("ind"))
    return jax.shard_map(
        local,
        mesh=mesh,
        in_specs=placed,
        out_specs=(P("var", "ind"), P("var", None)),
        check_vma=False,
    )
```

```python
import jax
import jax.numpy as jnp
from jax import lax
from jax.sharding import PartitionSpec as P

VARS_GENE = 4
NEED = 2
PAD_ROWS = 8
CHUNKS = 1


def split2(x):
    hi = lax.reduce_precision(x, exponent_bits=8, mantissa_bits=7)
    lo = x - hi
    return hi.astype(jnp.bfloat16), lo.astype(jnp.bfloat16)


def batched_tile_dot(lhs, tiles):
    cols = lhs.shape[1]
    parts = jnp.concatenate(split2(lhs), axis=1)
    prod = lax.dot_general(
        parts, tiles, (((2,), (2,)), ((0,), (0,))), preferred_element_type=jnp.float32
    )
    return prod[:, :cols] + prod[:, cols:]


def local(genotypes, variance_comp, grm_tiles, tile_rows, tile_cols, tile_live):
    cols_here, rows_here = genotypes.shape
    tile_size = grm_tiles.shape[1]
    slot_count = grm_tiles.shape[0]
    row_tiles = rows_here // tile_size
    off_count = slot_count - row_tiles
    me = lax.axis_index("ind")
    peers = lax.axis_size("ind")
    v = lax.axis_index("var")
    nvar = lax.axis_size("var")
    ncol = cols_here * nvar
    genes = ncol // VARS_GENE
    total_ind = peers * rows_here
    tau0 = variance_comp[0]
    tau1 = variance_comp[1]
    live = tile_live[0]

    eye = jnp.arange(tile_size)[:, None] == jnp.arange(tile_size)[None, :]
    diag_values = jnp.sum(
        jnp.where(eye[None], grm_tiles[:row_tiles].astype(jnp.float32), 0.0), axis=2
    )
    precond = (tau0 + tau1 * diag_values)[:, None, :]
    off_rows = tile_rows[row_tiles:]
    off_cols = tile_cols[row_tiles:]
    live_mask = (jnp.arange(row_tiles, slot_count, dtype=jnp.int32) < live).astype(jnp.float32)
    weight = (off_rows[:, None] == jnp.arange(row_tiles, dtype=jnp.int32)[None, :]).astype(jnp.float32)
    weight = weight * live_mask[:, None]
    position = off_cols // row_tiles * NEED + (off_cols % row_tiles - me) % row_tiles
    position = jnp.clip(position, 0, peers * NEED - 1)

    def to_tiles(x):
        return jnp.transpose(x.reshape(cols_here, row_tiles, tile_size), (1, 0, 2))

    def from_tiles(x):
        return jnp.transpose(x, (1, 0, 2)).reshape(cols_here, rows_here)

    def exchange(x, extra, by_concat=False):
        width = x.shape[1]
        if extra is None:
            rolled = jnp.stack([jnp.roll(x, -t, axis=0) for t in range(NEED)], axis=1)
            rolled = rolled.reshape(row_tiles, NEED * width, tile_size)
            pieces = jnp.tile(rolled, (peers // row_tiles, 1, 1))
            arrived = lax.all_to_all(pieces, "ind", split_axis=0, concat_axis=0, tiled=True)
            return arrived.reshape(peers * NEED, width, tile_size), None
        flat = extra.reshape(-1)
        flat = jnp.pad(flat, (0, PAD_ROWS * tile_size - flat.shape[0]))
        if by_concat:
            rows = []
            for p in range(peers):
                rows += [x[(p + t) % row_tiles] for t in range(NEED)]
                rows.append(flat.reshape(PAD_ROWS, tile_size))
            pieces = jnp.concatenate(rows, axis=0).reshape(peers, -1, tile_size)
        else:
            rolled = jnp.stack([jnp.roll(x, -t, axis=0) for t in range(NEED)], axis=1)
            rolled = rolled.reshape(row_tiles, NEED * width, tile_size)
            pieces = jnp.tile(rolled, (peers // row_tiles, 1, 1))
            side = jnp.broadcast_to(flat.reshape(1, PAD_ROWS, tile_size), (peers, PAD_ROWS, tile_size))
            pieces = jnp.concatenate([pieces, side], axis=1)
        arrived = lax.all_to_all(pieces, "ind", split_axis=0, concat_axis=0, tiled=True)
        tiles_in = arrived[:, :NEED * width].reshape(peers * NEED, width, tile_size)
        sums = jnp.sum(arrived[:, NEED * width:].reshape(peers, -1)[:, :extra.size], axis=0)
        return tiles_in, sums.reshape(extra.shape)

    def kprod(x, arrived, gather=False):
        width = x.shape[1]
        if gather:
            picked = jnp.take(arrived, position, axis=0, mode="clip")
        else:
            picked = jnp.stack([lax.dynamic_index_in_dim(arrived, position[s], 0, keepdims=False)
                                for s in range(off_count)])
        near = batched_tile_dot(x, grm_tiles[:row_tiles])
        far = batched_tile_dot(picked, grm_tiles[row_tiles:])
        return near + jnp.sum(weight[:, :, None, None] * far[:, None], axis=0)

    def colsum(x):
        return jnp.sum(x, axis=(0, 2))

    parts = [genotypes] + [
        lax.ppermute(genotypes, "var", [(j, (j + k) % nvar) for j in range(nvar)])
        for k in range(1, nvar)]
    parts = jnp.stack(parts)
    order = (v - jnp.arange(nvar, dtype=jnp.int32)) % nvar
    geno_all = jnp.take(parts, order, axis=0, mode="clip").reshape(ncol, rows_here)
    first = v * cols_here
    a_out = first // genes
    g0 = first % genes
    geno_sub = jnp.stack(
        [to_tiles(lax.dynamic_slice_in_dim(geno_all, a * genes + g0, cols_here, 0))
         for a in range(VARS_GENE)]
    )

    def chunk(g, geno_sub):
        z0 = g / precond
        tiles0, _ = exchange(z0, None)
        kz0 = kprod(z0, tiles0, gather=True)
        image0 = tau0 * z0 + tau1 * kz0
        w = image0 / precond
        p0_local = jnp.sum(geno_sub * z0[None], axis=(1, 3))
        extra1 = jnp.concatenate([colsum(g * z0)[None], colsum(z0 * image0)[None], p0_local], axis=0)
        tiles1, sums1 = exchange(w, extra1, by_concat=True)
        rz0 = sums1[0]
        dad0 = sums1[1]
        p0 = sums1[2:]
        alpha0 = rz0 / dad0
        resid1 = g - alpha0[None, :, None] * image0
        z1 = resid1 / precond
        kw = kprod(w, tiles1)
        kz1 = kz0 - alpha0[None, :, None] * kw
        az1 = tau0 * z1 + tau1 * kz1
        red_local = jnp.concatenate(
            [colsum(resid1 * z1)[None], colsum(z1 * az1)[None],
             colsum(z1 * image0 + z0 * az1)[None], jnp.sum(geno_sub * z1[None], axis=(1, 3))],
            axis=0,
        )
        lead = (me == 0).astype(jnp.float32)
        payload = jnp.concatenate(
            [red_local, lead * rz0[None], lead * dad0[None], lead * p0], axis=0)
        spread = jnp.broadcast_to(payload[None], (peers * nvar,) + payload.shape)
        got = lax.all_to_all(spread, ("ind", "var"), split_axis=0, concat_axis=0, tiled=True)
        tot = jnp.sum(got.reshape((peers, nvar) + payload.shape), axis=0)
        nv = VARS_GENE
        rz1_all = tot[:, 0]
        rz0_all = tot[:, 3 + nv]
        dad0_all = tot[:, 4 + nv]
        p0_all = tot[:, 5 + nv:]
        p1_all = tot[:, 3:3 + nv]
        alpha0_all = rz0_all / dad0_all
        beta_all = rz1_all / rz0_all
        dad1_all = tot[:, 1] + beta_all * (tot[:, 2] + beta_all * dad0_all)
        alpha1_all = rz1_all / dad1_all
        mine = lambda t: lax.dynamic_index_in_dim(t, v, 0, keepdims=False)
        beta = mine(beta_all)
        alpha1 = mine(alpha1_all)
        dir1 = z1 + beta[None, :, None] * z0
        sol = alpha0[None, :, None] * z0 + alpha1[None, :, None] * dir1
        part = alpha0_all[:, None] * p0_all + alpha1_all[:, None] * (p1_all + beta_all[:, None] * p0_all)
        return sol, part

    g_all = to_tiles(genotypes)
    width = cols_here // CHUNKS
    outs = [chunk(g_all[:, k * width:(k + 1) * width], geno_sub[:, :, k * width:(k + 1) * width])
            for k in range(CHUNKS)]
    solution = jnp.concatenate([o[0] for o in outs], axis=1)
    gram_part = jnp.concatenate([o[1] for o in outs], axis=2)
    full = jnp.transpose(gram_part, (1, 0, 2)).reshape(VARS_GENE, ncol)
    gram_cols = lax.dynamic_index_in_dim(full, a_out, 0, keepdims=False)
    gram_cols = lax.dynamic_slice_in_dim(gram_cols.reshape(VARS_GENE, genes), g0, cols_here, 1)
    gene_gram = jnp.transpose(gram_cols) / total_ind
    return (from_tiles(solution), gene_gram)


def solution(mesh):
    placed = (P("var", "ind"), P(), P("ind", None, None), P("ind"), P("ind"), P("ind"))
    return jax.shard_map(
        local,
        mesh=mesh,
        in_specs=placed,
        out_specs=(P("var", "ind"), P("var", None)),
        check_vma=False,
    )
```

```python
import jax
import jax.numpy as jnp
from jax import lax
from jax.sharding import PartitionSpec as P

VARS_GENE = 4
NEED = 2
PAD_ROWS = 8
CHUNKS = 1


def split2(x):
    hi = lax.reduce_precision(x, exponent_bits=8, mantissa_bits=7)
    lo = x - hi
    return hi.astype(jnp.bfloat16), lo.astype(jnp.bfloat16)


def batched_tile_dot(lhs, tiles):
    cols = lhs.shape[1]
    parts = jnp.concatenate(split2(lhs), axis=1)
    prod = lax.dot_general(
        parts, tiles, (((2,), (2,)), ((0,), (0,))), preferred_element_type=jnp.float32
    )
    return prod[:, :cols] + prod[:, cols:]


def local(genotypes, variance_comp, grm_tiles, tile_rows, tile_cols, tile_live):
    cols_here, rows_here = genotypes.shape
    tile_size = grm_tiles.shape[1]
    slot_count = grm_tiles.shape[0]
    row_tiles = rows_here // tile_size
    off_count = slot_count - row_tiles
    me = lax.axis_index("ind")
    peers = lax.axis_size("ind")
    v = lax.axis_index("var")
    nvar = lax.axis_size("var")
    ncol = cols_here * nvar
    genes = ncol // VARS_GENE
    total_ind = peers * rows_here
    tau0 = variance_comp[0]
    tau1 = variance_comp[1]
    live = tile_live[0]

    eye = jnp.arange(tile_size)[:, None] == jnp.arange(tile_size)[None, :]
    diag_values = jnp.sum(
        jnp.where(eye[None], grm_tiles[:row_tiles].astype(jnp.float32), 0.0), axis=2
    )
    precond = (tau0 + tau1 * diag_values)[:, None, :]
    off_rows = tile_rows[row_tiles:]
    off_cols = tile_cols[row_tiles:]
    live_mask = (jnp.arange(row_tiles, slot_count, dtype=jnp.int32) < live).astype(jnp.float32)
    weight = (off_rows[:, None] == jnp.arange(row_tiles, dtype=jnp.int32)[None, :]).astype(jnp.float32)
    weight = weight * live_mask[:, None]
    position = off_cols // row_tiles * NEED + (off_cols % row_tiles - me) % row_tiles
    position = jnp.clip(position, 0, peers * NEED - 1)

    def to_tiles(x):
        return jnp.transpose(x.reshape(cols_here, row_tiles, tile_size), (1, 0, 2))

    def from_tiles(x):
        return jnp.transpose(x, (1, 0, 2)).reshape(cols_here, rows_here)

    def exchange(x, extra, by_concat=False):
        width = x.shape[1]
        if extra is None:
            rolled = jnp.stack([jnp.roll(x, -t, axis=0) for t in range(NEED)], axis=1)
            rolled = rolled.reshape(row_tiles, NEED * width, tile_size)
            pieces = jnp.tile(rolled, (peers // row_tiles, 1, 1))
            arrived = lax.all_to_all(pieces, "ind", split_axis=0, concat_axis=0, tiled=True)
            return arrived.reshape(peers * NEED, width, tile_size), None
        flat = extra.reshape(-1)
        flat = jnp.pad(flat, (0, PAD_ROWS * tile_size - flat.shape[0]))
        if by_concat:
            rows = []
            for p in range(peers):
                rows += [x[(p + t) % row_tiles] for t in range(NEED)]
                rows.append(flat.reshape(PAD_ROWS, tile_size))
            pieces = jnp.concatenate(rows, axis=0).reshape(peers, -1, tile_size)
        else:
            rolled = jnp.stack([jnp.roll(x, -t, axis=0) for t in range(NEED)], axis=1)
            rolled = rolled.reshape(row_tiles, NEED * width, tile_size)
            pieces = jnp.tile(rolled, (peers // row_tiles, 1, 1))
            side = jnp.broadcast_to(flat.reshape(1, PAD_ROWS, tile_size), (peers, PAD_ROWS, tile_size))
            pieces = jnp.concatenate([pieces, side], axis=1)
        arrived = lax.all_to_all(pieces, "ind", split_axis=0, concat_axis=0, tiled=True)
        tiles_in = arrived[:, :NEED * width].reshape(peers * NEED, width, tile_size)
        sums = jnp.sum(arrived[:, NEED * width:].reshape(peers, -1)[:, :extra.size], axis=0)
        return tiles_in, sums.reshape(extra.shape)

    def kprod(x, arrived, gather=False):
        width = x.shape[1]
        if gather:
            pick = (position[:, None] == jnp.arange(arrived.shape[0], dtype=jnp.int32)[None, :])
            picked = jnp.einsum("sk,kct->sct", pick.astype(jnp.float32), arrived,
                                precision=lax.Precision.HIGHEST)
        else:
            picked = jnp.stack([lax.dynamic_index_in_dim(arrived, position[s], 0, keepdims=False)
                                for s in range(off_count)])
        near = batched_tile_dot(x, grm_tiles[:row_tiles])
        far = batched_tile_dot(picked, grm_tiles[row_tiles:])
        return near + jnp.sum(weight[:, :, None, None] * far[:, None], axis=0)

    def colsum(x):
        return jnp.sum(x, axis=(0, 2))

    parts = [genotypes] + [
        lax.ppermute(genotypes, "var", [(j, (j + k) % nvar) for j in range(nvar)])
        for k in range(1, nvar)]
    parts = jnp.stack(parts)
    order = (v - jnp.arange(nvar, dtype=jnp.int32)) % nvar
    geno_all = jnp.take(parts, order, axis=0, mode="clip").reshape(ncol, rows_here)
    first = v * cols_here
    a_out = first // genes
    g0 = first % genes
    geno_sub = jnp.stack(
        [to_tiles(lax.dynamic_slice_in_dim(geno_all, a * genes + g0, cols_here, 0))
         for a in range(VARS_GENE)]
    )

    def chunk(g, geno_sub):
        z0 = g / precond
        tiles0, _ = exchange(z0, None)
        kz0 = kprod(z0, tiles0, gather=True)
        image0 = tau0 * z0 + tau1 * kz0
        w = image0 / precond
        p0_local = jnp.sum(geno_sub * z0[None], axis=(1, 3))
        extra1 = jnp.concatenate([colsum(g * z0)[None], colsum(z0 * image0)[None], p0_local], axis=0)
        tiles1, sums1 = exchange(w, extra1, by_concat=True)
        rz0 = sums1[0]
        dad0 = sums1[1]
        p0 = sums1[2:]
        alpha0 = rz0 / dad0
        resid1 = g - alpha0[None, :, None] * image0
        z1 = resid1 / precond
        kw = kprod(w, tiles1)
        kz1 = kz0 - alpha0[None, :, None] * kw
        az1 = tau0 * z1 + tau1 * kz1
        red_local = jnp.concatenate(
            [colsum(resid1 * z1)[None], colsum(z1 * az1)[None],
             colsum(z1 * image0 + z0 * az1)[None], jnp.sum(geno_sub * z1[None], axis=(1, 3))],
            axis=0,
        )
        lead = (me == 0).astype(jnp.float32)
        payload = jnp.concatenate(
            [red_local, lead * rz0[None], lead * dad0[None], lead * p0], axis=0)
        spread = jnp.broadcast_to(payload[None], (peers * nvar,) + payload.shape)
        got = lax.all_to_all(spread, ("ind", "var"), split_axis=0, concat_axis=0, tiled=True)
        tot = jnp.sum(got.reshape((peers, nvar) + payload.shape), axis=0)
        nv = VARS_GENE
        rz1_all = tot[:, 0]
        rz0_all = tot[:, 3 + nv]
        dad0_all = tot[:, 4 + nv]
        p0_all = tot[:, 5 + nv:]
        p1_all = tot[:, 3:3 + nv]
        alpha0_all = rz0_all / dad0_all
        beta_all = rz1_all / rz0_all
        dad1_all = tot[:, 1] + beta_all * (tot[:, 2] + beta_all * dad0_all)
        alpha1_all = rz1_all / dad1_all
        mine = lambda t: lax.dynamic_index_in_dim(t, v, 0, keepdims=False)
        beta = mine(beta_all)
        alpha1 = mine(alpha1_all)
        dir1 = z1 + beta[None, :, None] * z0
        sol = alpha0[None, :, None] * z0 + alpha1[None, :, None] * dir1
        part = alpha0_all[:, None] * p0_all + alpha1_all[:, None] * (p1_all + beta_all[:, None] * p0_all)
        return sol, part

    g_all = to_tiles(genotypes)
    width = cols_here // CHUNKS
    outs = [chunk(g_all[:, k * width:(k + 1) * width], geno_sub[:, :, k * width:(k + 1) * width])
            for k in range(CHUNKS)]
    solution = jnp.concatenate([o[0] for o in outs], axis=1)
    gram_part = jnp.concatenate([o[1] for o in outs], axis=2)
    full = jnp.transpose(gram_part, (1, 0, 2)).reshape(VARS_GENE, ncol)
    gram_cols = lax.dynamic_index_in_dim(full, a_out, 0, keepdims=False)
    gram_cols = lax.dynamic_slice_in_dim(gram_cols.reshape(VARS_GENE, genes), g0, cols_here, 1)
    gene_gram = jnp.transpose(gram_cols) / total_ind
    return (from_tiles(solution), gene_gram)


def solution(mesh):
    placed = (P("var", "ind"), P(), P("ind", None, None), P("ind"), P("ind"), P("ind"))
    return jax.shard_map(
        local,
        mesh=mesh,
        in_specs=placed,
        out_specs=(P("var", "ind"), P("var", None)),
        check_vma=False,
    )
```
